32 devices in a mesh: groups: 2 (over y), row: 4 (over x, core), col: 4 (over z).
Axes of the slice: x: 2, y: 2, z: 4, core: 2. Of those that a mesh axis runs over, the one named last changes fastest.
Arguments:
- latent_in: bfloat16 [48, 16, 32, 640], P('groups', 'row', 'col'), parts along dimension 0, may hold values from -6 to 6
- cached_mid: bfloat16 [48, 16, 32, 640], P('groups', 'row', 'col'), parts along dimension 0, may hold values from -5 to 5
- cached_out: bfloat16 [48, 16, 32, 640], P('groups', 'row', 'col'), parts along dimension 0, may hold values from -6 to 6
- edit_tiles: int32 [48, 16], P('groups'), parts along dimension 0, may hold values from -1 to 31, as said below
- norm1_mean: float32 [48, 32], P('groups'), parts along dimension 0, may hold values from -2 to 2
- norm1_rstd: float32 [48, 32], P('groups'), parts along dimension 0, may hold values from 0.6 to 1.8
- norm1_gain: float32 [640], replicated, may hold values from 0.1 to 1.9
- norm1_shift: float32 [640], replicated, may hold values from -2 to 2
- conv1_weight: bfloat16 [3, 3, 640, 640], P(None, None, 'row'), may hold values from -0.078125 to 0.078125
- conv1_bias: float32 [640], replicated, may hold values from -2 to 2
- step_embed: float32 [48, 640], P('groups'), parts along dimension 0, may hold values from -3 to 3
- norm2_mean: float32 [48, 32], P('groups'), parts along dimension 0, may hold values from -1.5 to 1.5
- norm2_rstd: float32 [48, 32], P('groups'), parts along dimension 0, may hold values from 0.8 to 2.5
- norm2_gain: float32 [640], replicated, may hold values from 0.1 to 1.9
- norm2_shift: float32 [640], replicated, may hold values from -2 to 2
- conv2_weight: bfloat16 [3, 3, 640, 640], P(None, None, 'row'), may hold values from -0.078125 to 0.078125
- conv2_bias: float32 [640], replicated, may hold values from -2 to 2
Outputs:
- latent_out: bfloat16 [48, 16, 32, 640], P('groups', 'row', 'col'), parts along dimension 0
The draws below stay inside these ranges and needn't reach their ends.
There are 2 independent parts, one for each index of `groups`. The reference program is written for one: setup_inputs(seed, part) draws one part's arguments, and reference() takes and returns one part's arrays. A program takes and returns all parts, laid end to end along the dimension named above; an argument that names none is the same for every part. Nothing has to cross between parts.
Inputs may be any that keep to these rules, and one draw needn't show every extreme that they name: `edit_tiles`: each request lists, in increasing order, the tile numbers of one rectangle exactly 2 tile rows tall and 4 to 7 tile columns wide, then -1 to the end of the row.
All inputs are finite; a program needn't handle non-finite values.
Results may differ from the reference program's by a relative error of at most 0.0042.
Values may be sent and summed in bfloat16 or wider, within the bound.
No kernel may reach another device: no remote copies, remote signals or barrier semaphores. Data moves between devices by JAX's collectives and lax.ppermute only.
A program may use at most 128 MiB of HBM per device.

```python
import math
import jax
import jax.numpy as jnp
from jax import lax

C = 640
G = 32
TILE = 4
REQ = 24
TROWS = 4
TCOLS = 8
BOX = 2
LIST_LEN = 16
HEIGHT = 16
WIDTH = 32


def draw_edit_tiles(key, part):
    key_top = jax.random.fold_in(key, 11)
    key_width = jax.random.fold_in(key, 12)
    key_left = jax.random.fold_in(key, 13)
    window_top = jax.random.randint(key_top, (REQ,), 0, TROWS - BOX + 1)
    widths = jax.random.randint(key_width, (REQ,), TCOLS // 2, TCOLS)
    left_raw = jax.random.randint(key_left, (REQ,), 0, TCOLS)
    left_col = left_raw % (TCOLS - widths + 1)
    slots = jnp.arange(LIST_LEN, dtype=jnp.int32)
    box_row = slots[None, :] // widths[:, None]
    box_col = slots[None, :] % widths[:, None]
    tile_ids = (window_top[:, None] + box_row) * TCOLS + left_col[:, None] + box_col
    return jnp.where(box_row < BOX, tile_ids, -1).astype(jnp.int32)


def shard_levels(key, dims, pieces, least, top_value):
    def one(position, parts):
        steps = jax.random.uniform(jax.random.fold_in(jax.random.fold_in(key, 6), position), (parts,), jnp.float32, least / len(pieces), top_value / len(pieces))
        return jnp.repeat(jnp.exp(steps), dims[position] // parts).reshape((-1,) + (1,) * (len(dims) - position - 1))

    factor_of = one(*pieces[0])
    for cut in pieces[1:]:
        factor_of = factor_of * one(*cut)
    return factor_of


def centred(key, shape, width, limit, pieces=(), held_as=jnp.bfloat16):
    values = width * jax.random.normal(key, shape, jnp.float32)
    if pieces:
        values = values * shard_levels(key, shape, pieces, -0.22, 0.18)
    return jnp.clip(values, -limit, limit).astype(held_as)


def setup_inputs(seed: int = 0, part: int = 0) -> dict:
    key_of = jax.random.split(jax.random.key(seed), 18)
    own_keys = jax.random.split(jax.random.fold_in(key_of[17], part), 18)
    latent_in = centred(own_keys[0], (REQ, HEIGHT, WIDTH, C), 1.0, 6.0, ((1, 4), (2, 4)))
    cached_mid = centred(own_keys[1], (REQ, HEIGHT, WIDTH, C), 0.7, 5.0, ((1, 4), (2, 4)))
    cached_out = centred(own_keys[2], (REQ, HEIGHT, WIDTH, C), 1.0, 6.0, ((1, 4), (2, 4)))
    edit_tiles = draw_edit_tiles(jax.random.fold_in(jax.random.fold_in(key_of[17], part), 71), part)
    norm1_mean = centred(own_keys[4], (REQ, G), 0.4, 2.0, (), jnp.float32)
    norm1_rstd = jnp.clip(jnp.exp(jax.random.uniform(own_keys[5], (REQ, G), jnp.float32, math.log(0.6), math.log(1.8))), 0.6, 1.8)
    norm1_gain = jnp.clip(1.0 + 0.18 * jax.random.normal(key_of[6], (C,), jnp.float32), 0.1, 1.9)
    norm1_shift = centred(key_of[7], (C,), 0.4, 2.0, (), jnp.float32)
    conv1_weight = centred(key_of[8], (3, 3, C, C), (9 * C) ** -0.5, 0.078125, ((2, 4),))
    conv1_bias = centred(key_of[9], (C,), 0.4, 2.0, (), jnp.float32)
    step_embed = centred(own_keys[10], (REQ, C), 0.5, 3.0, (), jnp.float32)
    norm2_mean = centred(own_keys[11], (REQ, G), 0.3, 1.5, (), jnp.float32)
    norm2_rstd = jnp.clip(jnp.exp(jax.random.uniform(own_keys[12], (REQ, G), jnp.float32, math.log(0.8), math.log(2.5))), 0.8, 2.5)
    norm2_gain = jnp.clip(1.0 + 0.18 * jax.random.normal(key_of[13], (C,), jnp.float32), 0.1, 1.9)
    norm2_shift = centred(key_of[14], (C,), 0.4, 2.0, (), jnp.float32)
    conv2_weight = centred(key_of[15], (3, 3, C, C), (9 * C) ** -0.5, 0.078125, ((2, 4),))
    conv2_bias = centred(key_of[16], (C,), 0.4, 2.0, (), jnp.float32)
    return {"latent_in": latent_in, "cached_mid": cached_mid, "cached_out": cached_out, "edit_tiles": edit_tiles, "norm1_mean": norm1_mean, "norm1_rstd": norm1_rstd, "norm1_gain": norm1_gain, "norm1_shift": norm1_shift, "conv1_weight": conv1_weight, "conv1_bias": conv1_bias, "step_embed": step_embed, "norm2_mean": norm2_mean, "norm2_rstd": norm2_rstd, "norm2_gain": norm2_gain, "norm2_shift": norm2_shift, "conv2_weight": conv2_weight, "conv2_bias": conv2_bias}


def conv_taps(activation, kernel):
    tile_count = activation.shape[0]
    running = jnp.zeros((tile_count * TILE * TILE, C), jnp.float32)
    for tap_row in range(3):
        for tap_col in range(3):
            window = activation[:, tap_row:tap_row + TILE, tap_col:tap_col + TILE, :].reshape(-1, C)
            running = running + jnp.dot(window, kernel[tap_row, tap_col], preferred_element_type=jnp.float32)
    return running.reshape(tile_count, TILE, TILE, C)


def reference(latent_in, cached_mid, cached_out, edit_tiles, norm1_mean, norm1_rstd, norm1_gain, norm1_shift, conv1_weight, conv1_bias, step_embed, norm2_mean, norm2_rstd, norm2_gain, norm2_shift, conv2_weight, conv2_bias):
    block_tiles = 16
    edge_index = jnp.arange(TILE + 2, dtype=jnp.int32)
    edge_line = (edge_index == 0) | (edge_index == TILE + 1)
    margin_mask = (edge_line[:, None] | edge_line[None, :])[None, :, :, None]
    inside_map = jnp.pad(jnp.ones((HEIGHT, WIDTH), jnp.float32), 1)

    def one_request(request):
        stacked = jnp.pad(jnp.stack([latent_in[request], cached_mid[request]]), ((0, 0), (1, 1), (1, 1), (0, 0)))
        first_mean = jnp.repeat(norm1_mean[request], C // G)
        first_rstd = jnp.repeat(norm1_rstd[request], C // G)
        second_mean = jnp.repeat(norm2_mean[request], C // G)
        second_rstd = jnp.repeat(norm2_rstd[request], C // G)
        embedding = step_embed[request]

        def one_block(tile_ids):
            clipped = jnp.maximum(tile_ids, 0).astype(jnp.int32)

            def cut_patch(tile_row, tile_col):
                zero_index = jnp.zeros((), jnp.int32)
                start_row = (tile_row * TILE).astype(jnp.int32)
                start_col = (tile_col * TILE).astype(jnp.int32)
                tile_group = lax.dynamic_slice(stacked, (zero_index, start_row, start_col, zero_index), (2, TILE + 2, TILE + 2, C))
                border = lax.dynamic_slice(inside_map, (start_row, start_col), (TILE + 2, TILE + 2))
                return tile_group, border

            tile_group, border = jax.vmap(cut_patch)((clipped // TCOLS).astype(jnp.int32), (clipped % TCOLS).astype(jnp.int32))

            def compute_block():
                inputs = tile_group[:, 0].astype(jnp.float32)
                margins = tile_group[:, 1].astype(jnp.float32)
                first_act = (jax.nn.silu((inputs - first_mean) * first_rstd * norm1_gain + norm1_shift) * border[..., None]).astype(jnp.bfloat16)
                fresh_mid = conv_taps(first_act, conv1_weight) + conv1_bias + embedding
                middle = jnp.where(margin_mask, margins, jnp.pad(fresh_mid, ((0, 0), (1, 1), (1, 1), (0, 0))))
                second_act = (jax.nn.silu((middle - second_mean) * second_rstd * norm2_gain + norm2_shift) * border[..., None]).astype(jnp.bfloat16)
                return (conv_taps(second_act, conv2_weight) + conv2_bias + inputs[:, 1:1 + TILE, 1:1 + TILE]).astype(jnp.bfloat16)

            def skip_block():
                return jnp.zeros((block_tiles, TILE, TILE, C), jnp.bfloat16)

            return lax.cond(jnp.any(tile_ids >= 0), compute_block, skip_block)

        entries = edit_tiles[request]
        renewed = lax.map(one_block, entries.reshape(-1, block_tiles)).reshape(-1, TILE, TILE, C)
        out_tiles = cached_out[request].reshape(TROWS, TILE, TCOLS, TILE, C).transpose(0, 2, 1, 3, 4).reshape(TROWS * TCOLS, TILE, TILE, C)
        target = jnp.where(entries >= 0, entries, TROWS * TCOLS).astype(jnp.int32)
        out_tiles = out_tiles.at[target].set(renewed, mode="drop")
        return out_tiles.reshape(TROWS, TCOLS, TILE, TILE, C).transpose(0, 2, 1, 3, 4).reshape(HEIGHT, WIDTH, C)

    return lax.map(one_request, jnp.arange(REQ, dtype=jnp.int32))
```

```python
import jax
import jax.numpy as jnp
from jax import lax
from jax.sharding import PartitionSpec as P

TILE = 4


def padded_2(block, sides, width):
    for axis, dim in sides:
        count = lax.axis_size(axis)
        forward = [(i, i + 1) for i in range(count - 1)]
        backward = [(target, source) for source, target in forward]
        low = lax.ppermute(
            lax.slice_in_dim(block, block.shape[dim] - width, None, axis=dim), axis, forward
        )
        high = lax.ppermute(lax.slice_in_dim(block, 0, width, axis=dim), axis, backward)
        block = jnp.concatenate([low, block, high], axis=dim)
    return block


def gather_shards(shard, axis):
    count = lax.axis_size(axis)
    chips = count // 2
    me = lax.axis_index(axis)
    chip = me // 2
    core = me % 2
    mate_pairs = [(i, i ^ 1) for i in range(count)]
    pieces = [(shard, me), (lax.ppermute(shard, axis, mate_pairs), me + 1 - 2 * core)]
    for step in range(1, chips):
        pairs = [(((i // 2 + step) % chips) * 2 + i % 2, i) for i in range(count)]
        fetched = lax.ppermute(shard, axis, pairs)
        far_chip = (chip + step) % chips
        pieces.append((fetched, far_chip * 2 + core))
        pieces.append((lax.ppermute(fetched, axis, mate_pairs), far_chip * 2 + 1 - core))
    depth = shard.shape[2]
    whole = jnp.zeros(shard.shape[:2] + (depth * count,) + shard.shape[3:], shard.dtype)
    zero = jnp.zeros((), jnp.int32)
    for piece, source in pieces:
        whole = lax.dynamic_update_slice(
            whole, piece, (zero, zero, (source * depth).astype(jnp.int32), zero)
        )
    return whole


def conv_valid(activation, kernel):
    return lax.conv_general_dilated(
        activation,
        kernel,
        window_strides=(1, 1),
        padding="VALID",
        dimension_numbers=("NHWC", "HWIO", "NHWC"),
        preferred_element_type=jnp.float32,
    )


def body(
    latent_in,
    cached_mid,
    cached_out,
    edit_tiles,
    norm1_mean,
    norm1_rstd,
    norm1_gain,
    norm1_shift,
    conv1_weight,
    conv1_bias,
    step_embed,
    norm2_mean,
    norm2_rstd,
    norm2_gain,
    norm2_shift,
    conv2_weight,
    conv2_bias,
):
    requests, rows_dev, cols_dev, channels = latent_in.shape
    tiles_down = rows_dev // TILE
    tiles_across = cols_dev // TILE
    rows_total = rows_dev * lax.axis_size("row")
    cols_total = cols_dev * lax.axis_size("col")
    tile_cols_total = tiles_across * lax.axis_size("col")
    groups_total = norm1_mean.shape[1]
    per_group = channels // groups_total

    first_whole = gather_shards(conv1_weight, "row")
    second_whole = gather_shards(conv2_weight, "row")

    def expand(values):
        return jnp.repeat(values, per_group, axis=1)[:, None, None, :]

    stacked = jnp.stack([latent_in, cached_mid])
    padded = padded_2(stacked, (("row", 2), ("col", 3)), 1)
    inputs_pad = padded[0].astype(jnp.float32)
    margins_pad = padded[1].astype(jnp.float32)

    row_start = lax.axis_index("row") * rows_dev - 1
    col_start = lax.axis_index("col") * cols_dev - 1
    cell_rows = row_start + jnp.arange(rows_dev + 2, dtype=jnp.int32)
    cell_cols = col_start + jnp.arange(cols_dev + 2, dtype=jnp.int32)
    inside = ((cell_rows >= 0) & (cell_rows < rows_total))[:, None] & (
        (cell_cols >= 0) & (cell_cols < cols_total)
    )[None, :]
    inside = inside.astype(jnp.float32)[None, :, :, None]

    first_act = (
        jax.nn.silu(
            (inputs_pad - expand(norm1_mean)) * expand(norm1_rstd) * norm1_gain + norm1_shift
        )
        * inside
    ).astype(jnp.bfloat16)
    fresh_mid = (
        conv_valid(first_act, first_whole) + conv1_bias + step_embed[:, None, None, :]
    )

    windows = []
    masks = []
    for tile_down in range(tiles_down):
        for tile_across in range(tiles_across):
            r0 = tile_down * TILE
            c0 = tile_across * TILE
            margin = margins_pad[:, r0 : r0 + TILE + 2, c0 : c0 + TILE + 2]
            own = fresh_mid[:, r0 : r0 + TILE, c0 : c0 + TILE]
            windows.append(lax.dynamic_update_slice(margin, own, (0, 1, 1, 0)))
            masks.append(inside[:, r0 : r0 + TILE + 2, c0 : c0 + TILE + 2])
    middle = jnp.stack(windows, axis=1)
    border = jnp.stack(masks, axis=1)
    middle = middle.reshape((-1,) + middle.shape[2:])
    second_mean = expand(norm2_mean)[:, None]
    second_rstd = expand(norm2_rstd)[:, None]
    second_act = (
        jax.nn.silu(
            (middle.reshape((requests, -1) + middle.shape[1:]) - second_mean) * second_rstd
            * norm2_gain
            + norm2_shift
        )
        * border
    ).astype(jnp.bfloat16)
    second_act = second_act.reshape((-1,) + second_act.shape[2:])
    second_sum = conv_valid(second_act, second_whole)
    second_sum = second_sum.reshape(requests, tiles_down, tiles_across, TILE, TILE, channels)
    second_sum = jnp.transpose(second_sum, (0, 1, 3, 2, 4, 5)).reshape(
        requests, rows_dev, cols_dev, channels
    )
    renewed = (
        second_sum + conv2_bias + inputs_pad[:, 1 : 1 + rows_dev, 1 : 1 + cols_dev]
    ).astype(jnp.bfloat16)

    own_rows = lax.axis_index("row") * tiles_down + jnp.arange(tiles_down, dtype=jnp.int32)
    own_cols = lax.axis_index("col") * tiles_across + jnp.arange(tiles_across, dtype=jnp.int32)
    tile_numbers = own_rows[:, None] * tile_cols_total + own_cols[None, :]
    edited = jnp.any(edit_tiles[:, None, None, :] == tile_numbers[None, :, :, None], axis=-1)
    cell_mask = jnp.repeat(jnp.repeat(edited, TILE, axis=1), TILE, axis=2)
    return jnp.where(cell_mask[..., None], renewed, cached_out)


def solution(mesh):
    placed = (
        P("groups", "row", "col", None),
        P("groups", "row", "col", None),
        P("groups", "row", "col", None),
        P("groups", None),
        P("groups", None),
        P("groups", None),
        P(),
        P(),
        P(None, None, "row", None),
        P(),
        P("groups", None),
        P("groups", None),
        P("groups", None),
        P(),
        P(),
        P(None, None, "row", None),
        P(),
    )
    return jax.shard_map(
        body, mesh=mesh, in_specs=placed, out_specs=P("groups", "row", "col", None), check_vma=False
    )
```

```python
import jax
import jax.numpy as jnp
from jax import lax
from jax.sharding import PartitionSpec as P

TILE = 4


def padded_2(block, sides, width):
    for axis, dim in sides:
        count = lax.axis_size(axis)
        forward = [(i, i + 1) for i in range(count - 1)]
        backward = [(target, source) for source, target in forward]
        low = lax.ppermute(
            lax.slice_in_dim(block, block.shape[dim] - width, None, axis=dim), axis, forward
        )
        high = lax.ppermute(lax.slice_in_dim(block, 0, width, axis=dim), axis, backward)
        block = jnp.concatenate([low, block, high], axis=dim)
    return block


def gather_shards(shard):
    count = lax.axis_size("row")
    chips = count // 2
    plane = lax.axis_size("groups") * lax.axis_size("col")
    spot = lax.axis_index("groups") * lax.axis_size("col") + lax.axis_index("col")
    mate_pairs = [(i, i ^ 1) for i in range(count)]
    piece = lax.dynamic_slice_in_dim(shard.reshape(plane, -1), spot, 1, axis=0)
    local = [shard, lax.ppermute(shard, "row", mate_pairs)]
    remote = []
    for step in range(1, chips):
        pairs = [(((i // 2 + step) % chips) * 2 + i % 2, i) for i in range(count)]
        fetched = lax.ppermute(piece, "row", pairs)
        rebuilt = lax.all_gather(fetched, ("groups", "col"), axis=0, tiled=True)
        rebuilt = rebuilt.reshape(shard.shape)
        remote += [rebuilt, lax.ppermute(rebuilt, "row", mate_pairs)]
    return jnp.concatenate(local, axis=2), jnp.concatenate(remote, axis=2)


def relative_order(channels):
    count = lax.axis_size("row")
    chips = count // 2
    depth = channels // count
    me = lax.axis_index("row")
    chip = me // 2
    core = me % 2
    position = jnp.arange(channels, dtype=jnp.int32)
    block = position // depth
    source = 2 * ((chip + block // 2) % chips) + jnp.where(block % 2 == 0, core, 1 - core)
    return source * depth + position % depth


def conv_relative(activation, kernels, order):
    local_kernel, remote_kernel = kernels
    split = local_kernel.shape[2]
    natural = jnp.arange(activation.shape[-1], dtype=jnp.int32)[:, None]
    total = None
    for kernel, picks in ((local_kernel, order[:split]), (remote_kernel, order[split:])):
        chooser = (natural == picks[None, :]).astype(activation.dtype)
        part = jnp.dot(activation, chooser, preferred_element_type=jnp.float32)
        part = conv_valid(part.astype(activation.dtype), kernel)
        total = part if total is None else total + part
    return total


def conv_valid(activation, kernel):
    return lax.conv_general_dilated(
        activation,
        kernel,
        window_strides=(1, 1),
        padding="VALID",
        dimension_numbers=("NHWC", "HWIO", "NHWC"),
        preferred_element_type=jnp.float32,
    )


def body(
    latent_in,
    cached_mid,
    cached_out,
    edit_tiles,
    norm1_mean,
    norm1_rstd,
    norm1_gain,
    norm1_shift,
    conv1_weight,
    conv1_bias,
    step_embed,
    norm2_mean,
    norm2_rstd,
    norm2_gain,
    norm2_shift,
    conv2_weight,
    conv2_bias,
):
    requests, rows_dev, cols_dev, channels = latent_in.shape
    tiles_down = rows_dev // TILE
    tiles_across = cols_dev // TILE
    rows_total = rows_dev * lax.axis_size("row")
    cols_total = cols_dev * lax.axis_size("col")
    tile_cols_total = tiles_across * lax.axis_size("col")
    groups_total = norm1_mean.shape[1]
    per_group = channels // groups_total

    first_whole = gather_shards(conv1_weight)
    second_whole = gather_shards(conv2_weight)
    order = relative_order(channels)

    def expand(values):
        return jnp.repeat(values, per_group, axis=1)[:, None, None, :]

    stacked = jnp.stack([latent_in, cached_mid])
    padded = padded_2(stacked, (("row", 2), ("col", 3)), 1)
    inputs_pad = padded[0].astype(jnp.float32)
    margins_pad = padded[1].astype(jnp.float32)

    row_start = lax.axis_index("row") * rows_dev - 1
    col_start = lax.axis_index("col") * cols_dev - 1
    cell_rows = row_start + jnp.arange(rows_dev + 2, dtype=jnp.int32)
    cell_cols = col_start + jnp.arange(cols_dev + 2, dtype=jnp.int32)
    inside = ((cell_rows >= 0) & (cell_rows < rows_total))[:, None] & (
        (cell_cols >= 0) & (cell_cols < cols_total)
    )[None, :]
    inside = inside.astype(jnp.float32)[None, :, :, None]

    first_act = (
        jax.nn.silu(
            (inputs_pad - expand(norm1_mean)) * expand(norm1_rstd) * norm1_gain + norm1_shift
        )
        * inside
    ).astype(jnp.bfloat16)
    fresh_mid = (
        conv_relative(first_act, first_whole, order) + conv1_bias + step_embed[:, None, None, :]
    )

    windows = []
    masks = []
    for tile_down in range(tiles_down):
        for tile_across in range(tiles_across):
            r0 = tile_down * TILE
            c0 = tile_across * TILE
            margin = margins_pad[:, r0 : r0 + TILE + 2, c0 : c0 + TILE + 2]
            own = fresh_mid[:, r0 : r0 + TILE, c0 : c0 + TILE]
            windows.append(lax.dynamic_update_slice(margin, own, (0, 1, 1, 0)))
            masks.append(inside[:, r0 : r0 + TILE + 2, c0 : c0 + TILE + 2])
    middle = jnp.stack(windows, axis=1)
    border = jnp.stack(masks, axis=1)
    middle = middle.reshape((-1,) + middle.shape[2:])
    second_mean = expand(norm2_mean)[:, None]
    second_rstd = expand(norm2_rstd)[:, None]
    second_act = (
        jax.nn.silu(
            (middle.reshape((requests, -1) + middle.shape[1:]) - second_mean) * second_rstd
            * norm2_gain
            + norm2_shift
        )
        * border
    ).astype(jnp.bfloat16)
    second_act = second_act.reshape((-1,) + second_act.shape[2:])
    second_sum = conv_relative(second_act, second_whole, order)
    second_sum = second_sum.reshape(requests, tiles_down, tiles_across, TILE, TILE, channels)
    second_sum = jnp.transpose(second_sum, (0, 1, 3, 2, 4, 5)).reshape(
        requests, rows_dev, cols_dev, channels
    )
    renewed = (
        second_sum + conv2_bias + inputs_pad[:, 1 : 1 + rows_dev, 1 : 1 + cols_dev]
    ).astype(jnp.bfloat16)

    own_rows = lax.axis_index("row") * tiles_down + jnp.arange(tiles_down, dtype=jnp.int32)
    own_cols = lax.axis_index("col") * tiles_across + jnp.arange(tiles_across, dtype=jnp.int32)
    tile_numbers = own_rows[:, None] * tile_cols_total + own_cols[None, :]
    edited = jnp.any(edit_tiles[:, None, None, :] == tile_numbers[None, :, :, None], axis=-1)
    cell_mask = jnp.repeat(jnp.repeat(edited, TILE, axis=1), TILE, axis=2)
    return jnp.where(cell_mask[..., None], renewed, cached_out)


def solution(mesh):
    placed = (
        P("groups", "row", "col", None),
        P("groups", "row", "col", None),
        P("groups", "row", "col", None),
        P("groups", None),
        P("groups", None),
        P("groups", None),
        P(),
        P(),
        P(None, None, "row", None),
        P(),
        P("groups", None),
        P("groups", None),
        P("groups", None),
        P(),
        P(),
        P(None, None, "row", None),
        P(),
    )
    return jax.shard_map(
        body, mesh=mesh, in_specs=placed, out_specs=P("groups", "row", "col", None), check_vma=False
    )
```

```python
import jax
import jax.numpy as jnp
from jax import lax
from jax.sharding import PartitionSpec as P

TILE = 4


def padded_2(block, sides, width):
    for axis, dim in sides:
        count = lax.axis_size(axis)
        forward = [(i, i + 1) for i in range(count - 1)]
        backward = [(target, source) for source, target in forward]
        low = lax.ppermute(
            lax.slice_in_dim(block, block.shape[dim] - width, None, axis=dim), axis, forward
        )
        high = lax.ppermute(lax.slice_in_dim(block, 0, width, axis=dim), axis, backward)
        block = jnp.concatenate([low, block, high], axis=dim)
    return block


def quarter_index():
    return 2 * (lax.axis_index("groups") % 2) + lax.axis_index("col") % 2


def gather_shards(shard):
    count = lax.axis_size("row")
    chips = count // 2
    y_pairs = [(i, i ^ 1) for i in range(lax.axis_size("groups"))]
    z_pairs = [(i, i ^ 1) for i in range(lax.axis_size("col"))]
    mate_pairs = [(i, i ^ 1) for i in range(count)]
    depth = shard.shape[2]
    channels = shard.shape[3]
    lanes = ((channels // 2 + 127) // 128) * 128
    quarters = shard.reshape(shard.shape[:2] + (4, depth // 4, channels))
    mine = lax.dynamic_index_in_dim(quarters, quarter_index(), axis=2, keepdims=False)
    held = [shard, lax.ppermute(shard, "row", mate_pairs)]
    for step in range(1, chips):
        pairs = [(((i // 2 + step) % chips) * 2 + i % 2, i) for i in range(count)]
        fetched = lax.ppermute(mine, "row", pairs)
        from_z = lax.ppermute(fetched, "col", z_pairs)
        from_y = lax.ppermute(fetched, "groups", y_pairs)
        diagonal = jnp.concatenate(
            [
                lax.ppermute(from_z[..., :lanes], "groups", y_pairs),
                lax.ppermute(from_y[..., lanes:], "col", z_pairs),
            ],
            axis=3,
        )
        parts = [fetched, from_z, from_y, diagonal]
        relayed = [lax.ppermute(part, "row", mate_pairs) for part in parts]
        held += [jnp.concatenate(parts, axis=2), jnp.concatenate(relayed, axis=2)]
    return jnp.concatenate(held, axis=2)


def relative_order(channels):
    count = lax.axis_size("row")
    chips = count // 2
    depth = channels // count
    me = lax.axis_index("row")
    chip = me // 2
    core = me % 2
    position = jnp.arange(channels, dtype=jnp.int32)
    block = position // depth
    within = position % depth
    source = 2 * ((chip + block // 2) % chips) + jnp.where(block % 2 == 0, core, 1 - core)
    quarter = depth // 4
    shuffled = (quarter_index() ^ (within // quarter)) * quarter + within % quarter
    return source * depth + jnp.where(block >= 2, shuffled, within)


def conv_relative(activation, kernel, order):
    natural = jnp.arange(activation.shape[-1], dtype=jnp.int32)[:, None]
    chooser = (natural == order[None, :]).astype(activation.dtype)
    moved = jnp.dot(activation, chooser, preferred_element_type=jnp.float32)
    return conv_valid(moved.astype(activation.dtype), kernel)


def conv_valid(activation, kernel):
    return lax.conv_general_dilated(
        activation,
        kernel,
        window_strides=(1, 1),
        padding="VALID",
        dimension_numbers=("NHWC", "HWIO", "NHWC"),
        preferred_element_type=jnp.float32,
    )


def body(
    latent_in,
    cached_mid,
    cached_out,
    edit_tiles,
    norm1_mean,
    norm1_rstd,
    norm1_gain,
    norm1_shift,
    conv1_weight,
    conv1_bias,
    step_embed,
    norm2_mean,
    norm2_rstd,
    norm2_gain,
    norm2_shift,
    conv2_weight,
    conv2_bias,
):
    requests, rows_dev, cols_dev, channels = latent_in.shape
    tiles_down = rows_dev // TILE
    tiles_across = cols_dev // TILE
    rows_total = rows_dev * lax.axis_size("row")
    cols_total = cols_dev * lax.axis_size("col")
    tile_cols_total = tiles_across * lax.axis_size("col")
    groups_total = norm1_mean.shape[1]
    per_group = channels // groups_total

    first_whole = gather_shards(conv1_weight)
    second_whole = gather_shards(conv2_weight)
    order = relative_order(channels)

    def expand(values):
        return jnp.repeat(values, per_group, axis=1)[:, None, None, :]

    stacked = jnp.stack([latent_in, cached_mid])
    padded = padded_2(stacked, (("row", 2), ("col", 3)), 1)
    inputs_pad = padded[0].astype(jnp.float32)
    margins_pad = padded[1].astype(jnp.float32)

    row_start = lax.axis_index("row") * rows_dev - 1
    col_start = lax.axis_index("col") * cols_dev - 1
    cell_rows = row_start + jnp.arange(rows_dev + 2, dtype=jnp.int32)
    cell_cols = col_start + jnp.arange(cols_dev + 2, dtype=jnp.int32)
    inside = ((cell_rows >= 0) & (cell_rows < rows_total))[:, None] & (
        (cell_cols >= 0) & (cell_cols < cols_total)
    )[None, :]
    inside = inside.astype(jnp.float32)[None, :, :, None]

    first_act = (
        jax.nn.silu(
            (inputs_pad - expand(norm1_mean)) * expand(norm1_rstd) * norm1_gain + norm1_shift
        )
        * inside
    ).astype(jnp.bfloat16)
    fresh_mid = (
        conv_relative(first_act, first_whole, order) + conv1_bias + step_embed[:, None, None, :]
    )

    windows = []
    masks = []
    for tile_down in range(tiles_down):
        for tile_across in range(tiles_across):
            r0 = tile_down * TILE
            c0 = tile_across * TILE
            margin = margins_pad[:, r0 : r0 + TILE + 2, c0 : c0 + TILE + 2]
            own = fresh_mid[:, r0 : r0 + TILE, c0 : c0 + TILE]
            windows.append(lax.dynamic_update_slice(margin, own, (0, 1, 1, 0)))
            masks.append(inside[:, r0 : r0 + TILE + 2, c0 : c0 + TILE + 2])
    middle = jnp.stack(windows, axis=1)
    border = jnp.stack(masks, axis=1)
    middle = middle.reshape((-1,) + middle.shape[2:])
    second_mean = expand(norm2_mean)[:, None]
    second_rstd = expand(norm2_rstd)[:, None]
    second_act = (
        jax.nn.silu(
            (middle.reshape((requests, -1) + middle.shape[1:]) - second_mean) * second_rstd
            * norm2_gain
            + norm2_shift
        )
        * border
    ).astype(jnp.bfloat16)
    second_act = second_act.reshape((-1,) + second_act.shape[2:])
    second_sum = conv_relative(second_act, second_whole, order)
    second_sum = second_sum.reshape(requests, tiles_down, tiles_across, TILE, TILE, channels)
    second_sum = jnp.transpose(second_sum, (0, 1, 3, 2, 4, 5)).reshape(
        requests, rows_dev, cols_dev, channels
    )
    renewed = (
        second_sum + conv2_bias + inputs_pad[:, 1 : 1 + rows_dev, 1 : 1 + cols_dev]
    ).astype(jnp.bfloat16)

    own_rows = lax.axis_index("row") * tiles_down + jnp.arange(tiles_down, dtype=jnp.int32)
    own_cols = lax.axis_index("col") * tiles_across + jnp.arange(tiles_across, dtype=jnp.int32)
    tile_numbers = own_rows[:, None] * tile_cols_total + own_cols[None, :]
    edited = jnp.any(edit_tiles[:, None, None, :] == tile_numbers[None, :, :, None], axis=-1)
    cell_mask = jnp.repeat(jnp.repeat(edited, TILE, axis=1), TILE, axis=2)
    return jnp.where(cell_mask[..., None], renewed, cached_out)


def solution(mesh):
    placed = (
        P("groups", "row", "col", None),
        P("groups", "row", "col", None),
        P("groups", "row", "col", None),
        P("groups", None),
        P("groups", None),
        P("groups", None),
        P(),
        P(),
        P(None, None, "row", None),
        P(),
        P("groups", None),
        P("groups", None),
        P("groups", None),
        P(),
        P(),
        P(None, None, "row", None),
        P(),
    )
    return jax.shard_map(
        body, mesh=mesh, in_specs=placed, out_specs=P("groups", "row", "col", None), check_vma=False
    )
```

```python
import jax
import jax.numpy as jnp
from jax import lax
from jax.sharding import PartitionSpec as P

TILE = 4


def padded_2(block, sides, width):
    for axis, dim in sides:
        count = lax.axis_size(axis)
        forward = [(i, i + 1) for i in range(count - 1)]
        backward = [(target, source) for source, target in forward]
        low = lax.ppermute(
            lax.slice_in_dim(block, block.shape[dim] - width, None, axis=dim), axis, forward
        )
        high = lax.ppermute(lax.slice_in_dim(block, 0, width, axis=dim), axis, backward)
        block = jnp.concatenate([low, block, high], axis=dim)
    return block


def gather_weights(kernels):
    count = lax.axis_size("row")
    chips = count // 2
    y_pairs = [(i, i ^ 1) for i in range(lax.axis_size("groups"))]
    mate_pairs = [(i, i ^ 1) for i in range(count)]
    parity = lax.axis_index("groups") % 2
    mates = lax.ppermute(jnp.stack(kernels), "row", mate_pairs)
    wholes = []
    for index, shard in enumerate(kernels):
        depth = shard.shape[2]
        halves = shard.reshape(shard.shape[:2] + (2, depth // 2) + shard.shape[3:])
        mine = lax.dynamic_index_in_dim(halves, parity, axis=2, keepdims=False)
        held = [shard, mates[index]]
        for step in range(1, chips):
            pairs = [(((i // 2 + step) % chips) * 2 + i % 2, i) for i in range(count)]
            fetched = lax.ppermute(mine, "row", pairs)
            other = lax.ppermute(fetched, "groups", y_pairs)
            remote = jnp.concatenate([fetched, other], axis=2)
            held += [remote, lax.ppermute(remote, "row", mate_pairs)]
        wholes.append(jnp.concatenate(held, axis=2))
    return wholes


def relative_order(channels):
    count = lax.axis_size("row")
    chips = count // 2
    depth = channels // count
    me = lax.axis_index("row")
    chip = me // 2
    core = me % 2
    position = jnp.arange(channels, dtype=jnp.int32)
    block = position // depth
    within = position % depth
    source = 2 * ((chip + block // 2) % chips) + jnp.where(block % 2 == 0, core, 1 - core)
    half = depth // 2
    parity = lax.axis_index("groups") % 2
    shuffled = (parity ^ (within // half)) * half + within % half
    return source * depth + jnp.where(block >= 2, shuffled, within)


def conv_relative(activation, kernel, order):
    natural = jnp.arange(activation.shape[-1], dtype=jnp.int32)[:, None]
    chooser = (natural == order[None, :]).astype(activation.dtype)
    moved = jnp.dot(activation, chooser, preferred_element_type=jnp.float32)
    return conv_valid(moved.astype(activation.dtype), kernel)


def conv_valid(activation, kernel):
    return lax.conv_general_dilated(
        activation,
        kernel,
        window_strides=(1, 1),
        padding="VALID",
        dimension_numbers=("NHWC", "HWIO", "NHWC"),
        preferred_element_type=jnp.float32,
    )


def body(
    latent_in,
    cached_mid,
    cached_out,
    edit_tiles,
    norm1_mean,
    norm1_rstd,
    norm1_gain,
    norm1_shift,
    conv1_weight,
    conv1_bias,
    step_embed,
    norm2_mean,
    norm2_rstd,
    norm2_gain,
    norm2_shift,
    conv2_weight,
    conv2_bias,
):
    requests, rows_dev, cols_dev, channels = latent_in.shape
    tiles_down = rows_dev // TILE
    tiles_across = cols_dev // TILE
    rows_total = rows_dev * lax.axis_size("row")
    cols_total = cols_dev * lax.axis_size("col")
    tile_cols_total = tiles_across * lax.axis_size("col")
    groups_total = norm1_mean.shape[1]
    per_group = channels // groups_total

    first_whole, second_whole = gather_weights([conv1_weight, conv2_weight])
    order = relative_order(channels)

    def expand(values):
        return jnp.repeat(values, per_group, axis=1)[:, None, None, :]

    stacked = jnp.stack([latent_in, cached_mid])
    padded = padded_2(stacked, (("row", 2), ("col", 3)), 1)
    inputs_pad = padded[0].astype(jnp.float32)
    margins_pad = padded[1].astype(jnp.float32)

    row_start = lax.axis_index("row") * rows_dev - 1
    col_start = lax.axis_index("col") * cols_dev - 1
    cell_rows = row_start + jnp.arange(rows_dev + 2, dtype=jnp.int32)
    cell_cols = col_start + jnp.arange(cols_dev + 2, dtype=jnp.int32)
    inside = ((cell_rows >= 0) & (cell_rows < rows_total))[:, None] & (
        (cell_cols >= 0) & (cell_cols < cols_total)
    )[None, :]
    inside = inside.astype(jnp.float32)[None, :, :, None]

    first_act = (
        jax.nn.silu(
            (inputs_pad - expand(norm1_mean)) * expand(norm1_rstd) * norm1_gain + norm1_shift
        )
        * inside
    ).astype(jnp.bfloat16)
    fresh_mid = (
        conv_relative(first_act, first_whole, order) + conv1_bias + step_embed[:, None, None, :]
    )

    fresh_pad = jnp.pad(fresh_mid, ((0, 0), (1, 1), (1, 1), (0, 0)))
    edge = jnp.arange(TILE + 2, dtype=jnp.int32)
    interior = ((edge >= 1) & (edge <= TILE))[:, None] & ((edge >= 1) & (edge <= TILE))[None, :]
    interior = interior[None, :, :, None]
    windows = []
    masks = []
    for tile_down in range(tiles_down):
        for tile_across in range(tiles_across):
            r0 = tile_down * TILE
            c0 = tile_across * TILE
            cut = (slice(None), slice(r0, r0 + TILE + 2), slice(c0, c0 + TILE + 2))
            windows.append(jnp.where(interior, fresh_pad[cut], margins_pad[cut]))
            masks.append(inside[cut])
    middle = jnp.stack(windows, axis=1)
    border = jnp.stack(masks, axis=1)
    second_mean = expand(norm2_mean)[:, None]
    second_rstd = expand(norm2_rstd)[:, None]
    second_act = (
        jax.nn.silu((middle - second_mean) * second_rstd * norm2_gain + norm2_shift) * border
    ).astype(jnp.bfloat16)
    second_act = second_act.reshape((-1,) + second_act.shape[2:])
    second_sum = conv_relative(second_act, second_whole, order)
    second_sum = second_sum.reshape(requests, tiles_down, tiles_across, TILE, TILE, channels)
    second_sum = jnp.transpose(second_sum, (0, 1, 3, 2, 4, 5)).reshape(
        requests, rows_dev, cols_dev, channels
    )
    renewed = (
        second_sum + conv2_bias + inputs_pad[:, 1 : 1 + rows_dev, 1 : 1 + cols_dev]
    ).astype(jnp.bfloat16)

    own_rows = lax.axis_index("row") * tiles_down + jnp.arange(tiles_down, dtype=jnp.int32)
    own_cols = lax.axis_index("col") * tiles_across + jnp.arange(tiles_across, dtype=jnp.int32)
    tile_numbers = own_rows[:, None] * tile_cols_total + own_cols[None, :]
    edited = jnp.any(edit_tiles[:, None, None, :] == tile_numbers[None, :, :, None], axis=-1)
    cell_mask = jnp.repeat(jnp.repeat(edited, TILE, axis=1), TILE, axis=2)
    return jnp.where(cell_mask[..., None], renewed, cached_out)


def solution(mesh):
    placed = (
        P("groups", "row", "col", None),
        P("groups", "row", "col", None),
        P("groups", "row", "col", None),
        P("groups", None),
        P("groups", None),
        P("groups", None),
        P(),
        P(),
        P(None, None, "row", None),
        P(),
        P("groups", None),
        P("groups", None),
        P("groups", None),
        P(),
        P(),
        P(None, None, "row", None),
        P(),
    )
    return jax.shard_map(
        body, mesh=mesh, in_specs=placed, out_specs=P("groups", "row", "col", None), check_vma=False
    )
```

```python
import jax
import jax.numpy as jnp
from jax import lax
from jax.sharding import PartitionSpec as P

TILE = 4


def padded_2(block, sides, width):
    for axis, dim in sides:
        count = lax.axis_size(axis)
        forward = [(i, i + 1) for i in range(count - 1)]
        backward = [(target, source) for source, target in forward]
        low = lax.ppermute(
            lax.slice_in_dim(block, block.shape[dim] - width, None, axis=dim), axis, forward
        )
        high = lax.ppermute(lax.slice_in_dim(block, 0, width, axis=dim), axis, backward)
        block = jnp.concatenate([low, block, high], axis=dim)
    return block


def gather_weights(kernels):
    count = lax.axis_size("row")
    chips = count // 2
    y_pairs = [(i, i ^ 1) for i in range(lax.axis_size("groups"))]
    mate_pairs = [(i, i ^ 1) for i in range(count)]
    parity = lax.axis_index("groups") % 2
    wholes = []
    previous = None
    for shard in kernels:
        depth = shard.shape[2]
        halves = shard.reshape(shard.shape[:2] + (2, depth // 2) + shard.shape[3:])
        mine = lax.dynamic_index_in_dim(halves, parity, axis=2, keepdims=False)
        held = [shard, lax.ppermute(shard, "row", mate_pairs)]
        for step in range(1, chips):
            if previous is not None:
                mine, _ = lax.optimization_barrier((mine, previous))
            pairs = [(((i // 2 + step) % chips) * 2 + i % 2, i) for i in range(count)]
            fetched = lax.ppermute(mine, "row", pairs)
            previous = fetched
            other = lax.ppermute(fetched, "groups", y_pairs)
            relayed = lax.ppermute(fetched, "row", mate_pairs)
            other_relayed = lax.ppermute(other, "row", mate_pairs)
            held += [
                jnp.concatenate([fetched, other], axis=2),
                jnp.concatenate([relayed, other_relayed], axis=2),
            ]
        wholes.append(jnp.concatenate(held, axis=2))
    return wholes


def relative_order(channels):
    count = lax.axis_size("row")
    chips = count // 2
    depth = channels // count
    me = lax.axis_index("row")
    chip = me // 2
    core = me % 2
    position = jnp.arange(channels, dtype=jnp.int32)
    block = position // depth
    within = position % depth
    source = 2 * ((chip + block // 2) % chips) + jnp.where(block % 2 == 0, core, 1 - core)
    half = depth // 2
    parity = lax.axis_index("groups") % 2
    shuffled = (parity ^ (within // half)) * half + within % half
    return source * depth + jnp.where(block >= 2, shuffled, within)


def to_relative(activation, order):
    natural = jnp.arange(activation.shape[-1], dtype=jnp.int32)[:, None]
    chooser = (natural == order[None, :]).astype(activation.dtype)
    moved = jnp.dot(activation, chooser, preferred_element_type=jnp.float32)
    return moved.astype(activation.dtype)


def conv_relative(activation, kernel, order):
    return conv_valid(to_relative(activation, order), kernel)


def conv_valid(activation, kernel):
    return lax.conv_general_dilated(
        activation,
        kernel,
        window_strides=(1, 1),
        padding="VALID",
        dimension_numbers=("NHWC", "HWIO", "NHWC"),
        preferred_element_type=jnp.float32,
    )


def body(
    latent_in,
    cached_mid,
    cached_out,
    edit_tiles,
    norm1_mean,
    norm1_rstd,
    norm1_gain,
    norm1_shift,
    conv1_weight,
    conv1_bias,
    step_embed,
    norm2_mean,
    norm2_rstd,
    norm2_gain,
    norm2_shift,
    conv2_weight,
    conv2_bias,
):
    requests, rows_dev, cols_dev, channels = latent_in.shape
    tiles_down = rows_dev // TILE
    tiles_across = cols_dev // TILE
    rows_total = rows_dev * lax.axis_size("row")
    cols_total = cols_dev * lax.axis_size("col")
    tile_cols_total = tiles_across * lax.axis_size("col")
    groups_total = norm1_mean.shape[1]
    per_group = channels // groups_total

    first_whole, second_whole = gather_weights([conv1_weight, conv2_weight])
    order = relative_order(channels)

    def expand(values):
        return jnp.repeat(values, per_group, axis=1)[:, None, None, :]

    stacked = jnp.stack([latent_in, cached_mid])
    padded = padded_2(stacked, (("row", 2), ("col", 3)), 1)
    inputs_pad = padded[0].astype(jnp.float32)
    margins_pad = padded[1].astype(jnp.float32)

    row_start = lax.axis_index("row") * rows_dev - 1
    col_start = lax.axis_index("col") * cols_dev - 1
    cell_rows = row_start + jnp.arange(rows_dev + 2, dtype=jnp.int32)
    cell_cols = col_start + jnp.arange(cols_dev + 2, dtype=jnp.int32)
    inside = ((cell_rows >= 0) & (cell_rows < rows_total))[:, None] & (
        (cell_cols >= 0) & (cell_cols < cols_total)
    )[None, :]
    inside = inside.astype(jnp.float32)[None, :, :, None]

    first_act = (
        jax.nn.silu(
            (inputs_pad - expand(norm1_mean)) * expand(norm1_rstd) * norm1_gain + norm1_shift
        )
        * inside
    ).astype(jnp.bfloat16)
    fresh_mid = (
        conv_relative(first_act, first_whole, order) + conv1_bias + step_embed[:, None, None, :]
    )

    if tiles_down != 1:
        raise ValueError("tiles_down")
    second_mean = expand(norm2_mean)
    second_rstd = expand(norm2_rstd)

    def second_norm(values):
        return jax.nn.silu((values - second_mean) * second_rstd * norm2_gain + norm2_shift)

    cached_act = to_relative((second_norm(margins_pad) * inside).astype(jnp.bfloat16), order)
    fresh_act = to_relative(second_norm(fresh_mid).astype(jnp.bfloat16), order)
    blended = lax.dynamic_update_slice(cached_act, fresh_act, (0, 1, 1, 0))
    second_sum = conv_valid(blended, second_whole)
    fixes = jnp.zeros_like(second_sum)
    for boundary in range(1, tiles_across):
        edge_col = boundary * TILE
        for out_col, in_col, tap in ((edge_col - 1, edge_col + 1, 2), (edge_col, edge_col, 0)):
            pair = jnp.concatenate(
                [cached_act[:, :, in_col : in_col + 1], blended[:, :, in_col : in_col + 1]]
            )
            moved = conv_valid(pair, second_whole[:, tap : tap + 1])
            change = moved[:requests] - moved[requests:]
            fixes = fixes + jnp.pad(
                change, ((0, 0), (0, 0), (out_col, cols_dev - out_col - 1), (0, 0))
            )
    second_sum = second_sum + fixes
    renewed = (
        second_sum + conv2_bias + inputs_pad[:, 1 : 1 + rows_dev, 1 : 1 + cols_dev]
    ).astype(jnp.bfloat16)

    own_rows = lax.axis_index("row") * tiles_down + jnp.arange(tiles_down, dtype=jnp.int32)
    own_cols = lax.axis_index("col") * tiles_across + jnp.arange(tiles_across, dtype=jnp.int32)
    tile_numbers = own_rows[:, None] * tile_cols_total + own_cols[None, :]
    edited = jnp.any(edit_tiles[:, None, None, :] == tile_numbers[None, :, :, None], axis=-1)
    cell_mask = jnp.repeat(jnp.repeat(edited, TILE, axis=1), TILE, axis=2)
    return jnp.where(cell_mask[..., None], renewed, cached_out)


def solution(mesh):
    placed = (
        P("groups", "row", "col", None),
        P("groups", "row", "col", None),
        P("groups", "row", "col", None),
        P("groups", None),
        P("groups", None),
        P("groups", None),
        P(),
        P(),
        P(None, None, "row", None),
        P(),
        P("groups", None),
        P("groups", None),
        P("groups", None),
        P(),
        P(),
        P(None, None, "row", None),
        P(),
    )
    return jax.shard_map(
        body, mesh=mesh, in_specs=placed, out_specs=P("groups", "row", "col", None), check_vma=False
    )
```

```python
import jax
import jax.numpy as jnp
from jax import lax
from jax.sharding import PartitionSpec as P

TILE = 4


def padded_2(block, sides, width):
    for axis, dim in sides:
        count = lax.axis_size(axis)
        forward = [(i, i + 1) for i in range(count - 1)]
        backward = [(target, source) for source, target in forward]
        low = lax.ppermute(
            lax.slice_in_dim(block, block.shape[dim] - width, None, axis=dim), axis, forward
        )
        high = lax.ppermute(lax.slice_in_dim(block, 0, width, axis=dim), axis, backward)
        block = jnp.concatenate([low, block, high], axis=dim)
    return block


def gather_weights(kernels, swap_axes):
    count = lax.axis_size("row")
    chips = count // 2
    mate_pairs = [(i, i ^ 1) for i in range(count)]
    wholes = []
    previous = None
    for shard, swap_axis in zip(kernels, swap_axes):
        swap_pairs = [(i, i ^ 1) for i in range(lax.axis_size(swap_axis))]
        parity = lax.axis_index(swap_axis) % 2
        depth = shard.shape[2]
        halves = shard.reshape(shard.shape[:2] + (2, depth // 2) + shard.shape[3:])
        mine = lax.dynamic_index_in_dim(halves, parity, axis=2, keepdims=False)
        held = [shard, lax.ppermute(shard, "row", mate_pairs)]
        for step in range(1, chips):
            if previous is not None:
                mine, _ = lax.optimization_barrier((mine, previous))
            pairs = [(((i // 2 + step) % chips) * 2 + i % 2, i) for i in range(count)]
            fetched = lax.ppermute(mine, "row", pairs)
            previous = fetched
            other = lax.ppermute(fetched, swap_axis, swap_pairs)
            relayed = lax.ppermute(fetched, "row", mate_pairs)
            other_relayed = lax.ppermute(other, "row", mate_pairs)
            held += [
                jnp.concatenate([fetched, other], axis=2),
                jnp.concatenate([relayed, other_relayed], axis=2),
            ]
        wholes.append(jnp.concatenate(held, axis=2))
    return wholes


def relative_order(channels, swap_axis):
    count = lax.axis_size("row")
    chips = count // 2
    depth = channels // count
    me = lax.axis_index("row")
    chip = me // 2
    core = me % 2
    position = jnp.arange(channels, dtype=jnp.int32)
    block = position // depth
    within = position % depth
    source = 2 * ((chip + block // 2) % chips) + jnp.where(block % 2 == 0, core, 1 - core)
    half = depth // 2
    parity = lax.axis_index(swap_axis) % 2
    shuffled = (parity ^ (within // half)) * half + within % half
    return source * depth + jnp.where(block >= 2, shuffled, within)


def to_relative(activation, order):
    natural = jnp.arange(activation.shape[-1], dtype=jnp.int32)[:, None]
    chooser = (natural == order[None, :]).astype(activation.dtype)
    moved = jnp.dot(activation, chooser, preferred_element_type=jnp.float32)
    return moved.astype(activation.dtype)


def conv_relative(activation, kernel, order):
    return conv_valid(to_relative(activation, order), kernel)


def conv_valid(activation, kernel):
    return lax.conv_general_dilated(
        activation,
        kernel,
        window_strides=(1, 1),
        padding="VALID",
        dimension_numbers=("NHWC", "HWIO", "NHWC"),
        preferred_element_type=jnp.float32,
    )


def body(
    latent_in,
    cached_mid,
    cached_out,
    edit_tiles,
    norm1_mean,
    norm1_rstd,
    norm1_gain,
    norm1_shift,
    conv1_weight,
    conv1_bias,
    step_embed,
    norm2_mean,
    norm2_rstd,
    norm2_gain,
    norm2_shift,
    conv2_weight,
    conv2_bias,
):
    requests, rows_dev, cols_dev, channels = latent_in.shape
    tiles_down = rows_dev // TILE
    tiles_across = cols_dev // TILE
    rows_total = rows_dev * lax.axis_size("row")
    cols_total = cols_dev * lax.axis_size("col")
    tile_cols_total = tiles_across * lax.axis_size("col")
    groups_total = norm1_mean.shape[1]
    per_group = channels // groups_total

    first_whole, second_whole = gather_weights([conv1_weight, conv2_weight], ("groups", "col"))
    first_order = relative_order(channels, "groups")
    order = relative_order(channels, "col")

    def expand(values):
        return jnp.repeat(values, per_group, axis=1)[:, None, None, :]

    stacked = jnp.stack([latent_in, cached_mid])
    padded = padded_2(stacked, (("row", 2), ("col", 3)), 1)
    inputs_pad = padded[0].astype(jnp.float32)
    margins_pad = padded[1].astype(jnp.float32)

    row_start = lax.axis_index("row") * rows_dev - 1
    col_start = lax.axis_index("col") * cols_dev - 1
    cell_rows = row_start + jnp.arange(rows_dev + 2, dtype=jnp.int32)
    cell_cols = col_start + jnp.arange(cols_dev + 2, dtype=jnp.int32)
    inside = ((cell_rows >= 0) & (cell_rows < rows_total))[:, None] & (
        (cell_cols >= 0) & (cell_cols < cols_total)
    )[None, :]
    inside = inside.astype(jnp.float32)[None, :, :, None]

    first_act = (
        jax.nn.silu(
            (inputs_pad - expand(norm1_mean)) * expand(norm1_rstd) * norm1_gain + norm1_shift
        )
        * inside
    ).astype(jnp.bfloat16)
    fresh_mid = (
        conv_relative(first_act, first_whole, first_order) + conv1_bias + step_embed[:, None, None, :]
    )

    if tiles_down != 1:
        raise ValueError("tiles_down")
    second_mean = expand(norm2_mean)
    second_rstd = expand(norm2_rstd)

    def second_norm(values):
        return jax.nn.silu((values - second_mean) * second_rstd * norm2_gain + norm2_shift)

    cached_act = to_relative((second_norm(margins_pad) * inside).astype(jnp.bfloat16), order)
    fresh_act = to_relative(second_norm(fresh_mid).astype(jnp.bfloat16), order)
    blended = lax.dynamic_update_slice(cached_act, fresh_act, (0, 1, 1, 0))
    second_sum = conv_valid(blended, second_whole)
    fixes = jnp.zeros_like(second_sum)
    for boundary in range(1, tiles_across):
        edge_col = boundary * TILE
        for out_col, in_col, tap in ((edge_col - 1, edge_col + 1, 2), (edge_col, edge_col, 0)):
            pair = jnp.concatenate(
                [cached_act[:, :, in_col : in_col + 1], blended[:, :, in_col : in_col + 1]]
            )
            moved = conv_valid(pair, second_whole[:, tap : tap + 1])
            change = moved[:requests] - moved[requests:]
            fixes = fixes + jnp.pad(
                change, ((0, 0), (0, 0), (out_col, cols_dev - out_col - 1), (0, 0))
            )
    second_sum = second_sum + fixes
    renewed = (
        second_sum + conv2_bias + inputs_pad[:, 1 : 1 + rows_dev, 1 : 1 + cols_dev]
    ).astype(jnp.bfloat16)

    own_rows = lax.axis_index("row") * tiles_down + jnp.arange(tiles_down, dtype=jnp.int32)
    own_cols = lax.axis_index("col") * tiles_across + jnp.arange(tiles_across, dtype=jnp.int32)
    tile_numbers = own_rows[:, None] * tile_cols_total + own_cols[None, :]
    edited = jnp.any(edit_tiles[:, None, None, :] == tile_numbers[None, :, :, None], axis=-1)
    cell_mask = jnp.repeat(jnp.repeat(edited, TILE, axis=1), TILE, axis=2)
    return jnp.where(cell_mask[..., None], renewed, cached_out)


def solution(mesh):
    placed = (
        P("groups", "row", "col", None),
        P("groups", "row", "col", None),
        P("groups", "row", "col", None),
        P("groups", None),
        P("groups", None),
        P("groups", None),
        P(),
        P(),
        P(None, None, "row", None),
        P(),
        P("groups", None),
        P("groups", None),
        P("groups", None),
        P(),
        P(),
        P(None, None, "row", None),
        P(),
    )
    return jax.shard_map(
        body, mesh=mesh, in_specs=placed, out_specs=P("groups", "row", "col", None), check_vma=False
    )
```

```python
import jax
import jax.numpy as jnp
from jax import lax
from jax.sharding import PartitionSpec as P

TILE = 4


def padded_2(block, sides, width):
    for axis, dim in sides:
        count = lax.axis_size(axis)
        forward = [(i, i + 1) for i in range(count - 1)]
        backward = [(target, source) for source, target in forward]
        low = lax.ppermute(
            lax.slice_in_dim(block, block.shape[dim] - width, None, axis=dim), axis, forward
        )
        high = lax.ppermute(lax.slice_in_dim(block, 0, width, axis=dim), axis, backward)
        block = jnp.concatenate([low, block, high], axis=dim)
    return block


def gather_weights(kernels, swap_axes):
    count = lax.axis_size("row")
    chips = count // 2
    mate_pairs = [(i, i ^ 1) for i in range(count)]
    wholes = []
    for shard, swap_axis in zip(kernels, swap_axes):
        swap_pairs = [(i, i ^ 1) for i in range(lax.axis_size(swap_axis))]
        parity = lax.axis_index(swap_axis) % 2
        depth = shard.shape[2]
        halves = shard.reshape(shard.shape[:2] + (2, depth // 2) + shard.shape[3:])
        mine = lax.dynamic_index_in_dim(halves, parity, axis=2, keepdims=False)
        held = [shard, lax.ppermute(shard, "row", mate_pairs)]
        for step in range(1, chips):
            pairs = [(((i // 2 + step) % chips) * 2 + i % 2, i) for i in range(count)]
            fetched = lax.ppermute(mine, "row", pairs)
            other = lax.ppermute(fetched, swap_axis, swap_pairs)
            relayed = lax.ppermute(fetched, "row", mate_pairs)
            other_relayed = lax.ppermute(other, "row", mate_pairs)
            held += [
                jnp.concatenate([fetched, other], axis=2),
                jnp.concatenate([relayed, other_relayed], axis=2),
            ]
        wholes.append(jnp.concatenate(held, axis=2))
    return wholes


def relative_order(channels, swap_axis):
    count = lax.axis_size("row")
    chips = count // 2
    depth = channels // count
    me = lax.axis_index("row")
    chip = me // 2
    core = me % 2
    position = jnp.arange(channels, dtype=jnp.int32)
    block = position // depth
    within = position % depth
    source = 2 * ((chip + block // 2) % chips) + jnp.where(block % 2 == 0, core, 1 - core)
    half = depth // 2
    parity = lax.axis_index(swap_axis) % 2
    shuffled = (parity ^ (within // half)) * half + within % half
    return source * depth + jnp.where(block >= 2, shuffled, within)


def to_relative(activation, order):
    natural = jnp.arange(activation.shape[-1], dtype=jnp.int32)[:, None]
    chooser = (natural == order[None, :]).astype(activation.dtype)
    moved = jnp.dot(activation, chooser, preferred_element_type=jnp.float32)
    return moved.astype(activation.dtype)


def conv_relative(activation, kernel, order):
    return conv_valid(to_relative(activation, order), kernel)


def conv_valid(activation, kernel):
    return lax.conv_general_dilated(
        activation,
        kernel,
        window_strides=(1, 1),
        padding="VALID",
        dimension_numbers=("NHWC", "HWIO", "NHWC"),
        preferred_element_type=jnp.float32,
    )


def body(
    latent_in,
    cached_mid,
    cached_out,
    edit_tiles,
    norm1_mean,
    norm1_rstd,
    norm1_gain,
    norm1_shift,
    conv1_weight,
    conv1_bias,
    step_embed,
    norm2_mean,
    norm2_rstd,
    norm2_gain,
    norm2_shift,
    conv2_weight,
    conv2_bias,
):
    requests, rows_dev, cols_dev, channels = latent_in.shape
    tiles_down = rows_dev // TILE
    tiles_across = cols_dev // TILE
    rows_total = rows_dev * lax.axis_size("row")
    cols_total = cols_dev * lax.axis_size("col")
    tile_cols_total = tiles_across * lax.axis_size("col")
    groups_total = norm1_mean.shape[1]
    per_group = channels // groups_total

    first_whole, second_whole = gather_weights([conv1_weight, conv2_weight], ("groups", "col"))
    first_order = relative_order(channels, "groups")
    order = relative_order(channels, "col")

    def expand(values):
        return jnp.repeat(values, per_group, axis=1)[:, None, None, :]

    stacked = jnp.stack([latent_in, cached_mid])
    padded = padded_2(stacked, (("row", 2), ("col", 3)), 1)
    inputs_pad = padded[0].astype(jnp.float32)
    margins_pad = padded[1].astype(jnp.float32)

    row_start = lax.axis_index("row") * rows_dev - 1
    col_start = lax.axis_index("col") * cols_dev - 1
    cell_rows = row_start + jnp.arange(rows_dev + 2, dtype=jnp.int32)
    cell_cols = col_start + jnp.arange(cols_dev + 2, dtype=jnp.int32)
    inside = ((cell_rows >= 0) & (cell_rows < rows_total))[:, None] & (
        (cell_cols >= 0) & (cell_cols < cols_total)
    )[None, :]
    inside = inside.astype(jnp.float32)[None, :, :, None]

    first_act = (
        jax.nn.silu(
            (inputs_pad - expand(norm1_mean)) * expand(norm1_rstd) * norm1_gain + norm1_shift
        )
        * inside
    ).astype(jnp.bfloat16)
    fresh_mid = (
        conv_relative(first_act, first_whole, first_order) + conv1_bias + step_embed[:, None, None, :]
    )

    if tiles_down != 1:
        raise ValueError("tiles_down")
    second_mean = expand(norm2_mean)
    second_rstd = expand(norm2_rstd)

    def second_norm(values):
        return jax.nn.silu((values - second_mean) * second_rstd * norm2_gain + norm2_shift)

    cached_act = to_relative((second_norm(margins_pad) * inside).astype(jnp.bfloat16), order)
    fresh_act = to_relative(second_norm(fresh_mid).astype(jnp.bfloat16), order)
    blended = lax.dynamic_update_slice(cached_act, fresh_act, (0, 1, 1, 0))
    second_sum = conv_valid(blended, second_whole)
    fixes = jnp.zeros_like(second_sum)
    for boundary in range(1, tiles_across):
        edge_col = boundary * TILE
        for out_col, in_col, tap in ((edge_col - 1, edge_col + 1, 2), (edge_col, edge_col, 0)):
            pair = jnp.concatenate(
                [cached_act[:, :, in_col : in_col + 1], blended[:, :, in_col : in_col + 1]]
            )
            moved = conv_valid(pair, second_whole[:, tap : tap + 1])
            change = moved[:requests] - moved[requests:]
            fixes = fixes + jnp.pad(
                change, ((0, 0), (0, 0), (out_col, cols_dev - out_col - 1), (0, 0))
            )
    second_sum = second_sum + fixes
    renewed = (
        second_sum + conv2_bias + inputs_pad[:, 1 : 1 + rows_dev, 1 : 1 + cols_dev]
    ).astype(jnp.bfloat16)

    own_rows = lax.axis_index("row") * tiles_down + jnp.arange(tiles_down, dtype=jnp.int32)
    own_cols = lax.axis_index("col") * tiles_across + jnp.arange(tiles_across, dtype=jnp.int32)
    tile_numbers = own_rows[:, None] * tile_cols_total + own_cols[None, :]
    edited = jnp.any(edit_tiles[:, None, None, :] == tile_numbers[None, :, :, None], axis=-1)
    cell_mask = jnp.repeat(jnp.repeat(edited, TILE, axis=1), TILE, axis=2)
    return jnp.where(cell_mask[..., None], renewed, cached_out)


def solution(mesh):
    placed = (
        P("groups", "row", "col", None),
        P("groups", "row", "col", None),
        P("groups", "row", "col", None),
        P("groups", None),
        P("groups", None),
        P("groups", None),
        P(),
        P(),
        P(None, None, "row", None),
        P(),
        P("groups", None),
        P("groups", None),
        P("groups", None),
        P(),
        P(),
        P(None, None, "row", None),
        P(),
    )
    return jax.shard_map(
        body, mesh=mesh, in_specs=placed, out_specs=P("groups", "row", "col", None), check_vma=False
    )
```

```python
import jax
import jax.numpy as jnp
from jax import lax
from jax.sharding import PartitionSpec as P

TILE = 4


def padded_2(block, sides, width):
    for axis, dim in sides:
        count = lax.axis_size(axis)
        forward = [(i, i + 1) for i in range(count - 1)]
        backward = [(target, source) for source, target in forward]
        low = lax.ppermute(
            lax.slice_in_dim(block, block.shape[dim] - width, None, axis=dim), axis, forward
        )
        high = lax.ppermute(lax.slice_in_dim(block, 0, width, axis=dim), axis, backward)
        block = jnp.concatenate([low, block, high], axis=dim)
    return block


def gather_weights(kernels, swap_axes):
    count = lax.axis_size("row")
    chips = count // 2
    mate_pairs = [(i, i ^ 1) for i in range(count)]
    mates = lax.ppermute(jnp.stack(kernels), "row", mate_pairs)
    mine = []
    for shard, swap_axis in zip(kernels, swap_axes):
        depth = shard.shape[2]
        halves = shard.reshape(shard.shape[:2] + (2, depth // 2) + shard.shape[3:])
        parity = lax.axis_index(swap_axis) % 2
        mine.append(lax.dynamic_index_in_dim(halves, parity, axis=2, keepdims=False))
    mine = jnp.stack(mine)
    held = [[shard, mates[index]] for index, shard in enumerate(kernels)]
    for step in range(1, chips):
        pairs = [(((i // 2 + step) % chips) * 2 + i % 2, i) for i in range(count)]
        fetched = lax.ppermute(mine, "row", pairs)
        relayed = lax.ppermute(fetched, "row", mate_pairs)
        for index, swap_axis in enumerate(swap_axes):
            swap_pairs = [(i, i ^ 1) for i in range(lax.axis_size(swap_axis))]
            other = lax.ppermute(fetched[index], swap_axis, swap_pairs)
            other_relayed = lax.ppermute(other, "row", mate_pairs)
            held[index] += [
                jnp.concatenate([fetched[index], other], axis=2),
                jnp.concatenate([relayed[index], other_relayed], axis=2),
            ]
    return [jnp.concatenate(pieces, axis=2) for pieces in held]


def relative_order(channels, swap_axis):
    count = lax.axis_size("row")
    chips = count // 2
    depth = channels // count
    me = lax.axis_index("row")
    chip = me // 2
    core = me % 2
    position = jnp.arange(channels, dtype=jnp.int32)
    block = position // depth
    within = position % depth
    source = 2 * ((chip + block // 2) % chips) + jnp.where(block % 2 == 0, core, 1 - core)
    half = depth // 2
    parity = lax.axis_index(swap_axis) % 2
    shuffled = (parity ^ (within // half)) * half + within % half
    return source * depth + jnp.where(block >= 2, shuffled, within)


def to_relative(activation, order):
    natural = jnp.arange(activation.shape[-1], dtype=jnp.int32)[:, None]
    chooser = (natural == order[None, :]).astype(activation.dtype)
    moved = jnp.dot(activation, chooser, preferred_element_type=jnp.float32)
    return moved.astype(activation.dtype)


def conv_relative(activation, kernel, order):
    return conv_valid(to_relative(activation, order), kernel)


def conv_valid(activation, kernel):
    return lax.conv_general_dilated(
        activation,
        kernel,
        window_strides=(1, 1),
        padding="VALID",
        dimension_numbers=("NHWC", "HWIO", "NHWC"),
        preferred_element_type=jnp.float32,
    )


def body(
    latent_in,
    cached_mid,
    cached_out,
    edit_tiles,
    norm1_mean,
    norm1_rstd,
    norm1_gain,
    norm1_shift,
    conv1_weight,
    conv1_bias,
    step_embed,
    norm2_mean,
    norm2_rstd,
    norm2_gain,
    norm2_shift,
    conv2_weight,
    conv2_bias,
):
    requests, rows_dev, cols_dev, channels = latent_in.shape
    tiles_down = rows_dev // TILE
    tiles_across = cols_dev // TILE
    rows_total = rows_dev * lax.axis_size("row")
    cols_total = cols_dev * lax.axis_size("col")
    tile_cols_total = tiles_across * lax.axis_size("col")
    groups_total = norm1_mean.shape[1]
    per_group = channels // groups_total

    first_whole, second_whole = gather_weights([conv1_weight, conv2_weight], ("groups", "col"))
    first_order = relative_order(channels, "groups")
    order = relative_order(channels, "col")

    def expand(values):
        return jnp.repeat(values, per_group, axis=1)[:, None, None, :]

    stacked = jnp.stack([latent_in, cached_mid])
    padded = padded_2(stacked, (("row", 2), ("col", 3)), 1)
    inputs_pad = padded[0].astype(jnp.float32)
    margins_pad = padded[1].astype(jnp.float32)

    row_start = lax.axis_index("row") * rows_dev - 1
    col_start = lax.axis_index("col") * cols_dev - 1
    cell_rows = row_start + jnp.arange(rows_dev + 2, dtype=jnp.int32)
    cell_cols = col_start + jnp.arange(cols_dev + 2, dtype=jnp.int32)
    inside = ((cell_rows >= 0) & (cell_rows < rows_total))[:, None] & (
        (cell_cols >= 0) & (cell_cols < cols_total)
    )[None, :]
    inside = inside.astype(jnp.float32)[None, :, :, None]

    first_act = (
        jax.nn.silu(
            (inputs_pad - expand(norm1_mean)) * expand(norm1_rstd) * norm1_gain + norm1_shift
        )
        * inside
    ).astype(jnp.bfloat16)
    fresh_mid = (
        conv_relative(first_act, first_whole, first_order) + conv1_bias + step_embed[:, None, None, :]
    )

    if tiles_down != 1:
        raise ValueError("tiles_down")
    second_mean = expand(norm2_mean)
    second_rstd = expand(norm2_rstd)

    def second_norm(values):
        return jax.nn.silu((values - second_mean) * second_rstd * norm2_gain + norm2_shift)

    cached_act = to_relative((second_norm(margins_pad) * inside).astype(jnp.bfloat16), order)
    fresh_act = to_relative(second_norm(fresh_mid).astype(jnp.bfloat16), order)
    blended = lax.dynamic_update_slice(cached_act, fresh_act, (0, 1, 1, 0))
    second_sum = conv_valid(blended, second_whole)
    fixes = jnp.zeros_like(second_sum)
    for boundary in range(1, tiles_across):
        edge_col = boundary * TILE
        for out_col, in_col, tap in ((edge_col - 1, edge_col + 1, 2), (edge_col, edge_col, 0)):
            pair = jnp.concatenate(
                [cached_act[:, :, in_col : in_col + 1], blended[:, :, in_col : in_col + 1]]
            )
            moved = conv_valid(pair, second_whole[:, tap : tap + 1])
            change = moved[:requests] - moved[requests:]
            fixes = fixes + jnp.pad(
                change, ((0, 0), (0, 0), (out_col, cols_dev - out_col - 1), (0, 0))
            )
    second_sum = second_sum + fixes
    renewed = (
        second_sum + conv2_bias + inputs_pad[:, 1 : 1 + rows_dev, 1 : 1 + cols_dev]
    ).astype(jnp.bfloat16)

    own_rows = lax.axis_index("row") * tiles_down + jnp.arange(tiles_down, dtype=jnp.int32)
    own_cols = lax.axis_index("col") * tiles_across + jnp.arange(tiles_across, dtype=jnp.int32)
    tile_numbers = own_rows[:, None] * tile_cols_total + own_cols[None, :]
    edited = jnp.any(edit_tiles[:, None, None, :] == tile_numbers[None, :, :, None], axis=-1)
    cell_mask = jnp.repeat(jnp.repeat(edited, TILE, axis=1), TILE, axis=2)
    return jnp.where(cell_mask[..., None], renewed, cached_out)


def solution(mesh):
    placed = (
        P("groups", "row", "col", None),
        P("groups", "row", "col", None),
        P("groups", "row", "col", None),
        P("groups", None),
        P("groups", None),
        P("groups", None),
        P(),
        P(),
        P(None, None, "row", None),
        P(),
        P("groups", None),
        P("groups", None),
        P("groups", None),
        P(),
        P(),
        P(None, None, "row", None),
        P(),
    )
    return jax.shard_map(
        body, mesh=mesh, in_specs=placed, out_specs=P("groups", "row", "col", None), check_vma=False
    )
```

```python
import jax
import jax.numpy as jnp
from jax import lax
from jax.sharding import PartitionSpec as P

TILE = 4


def padded_2(block, sides, width):
    for axis, dim in sides:
        count = lax.axis_size(axis)
        forward = [(i, i + 1) for i in range(count - 1)]
        backward = [(target, source) for source, target in forward]
        low = lax.ppermute(
            lax.slice_in_dim(block, block.shape[dim] - width, None, axis=dim), axis, forward
        )
        high = lax.ppermute(lax.slice_in_dim(block, 0, width, axis=dim), axis, backward)
        block = jnp.concatenate([low, block, high], axis=dim)
    return block


def gather_weights(kernels, swap_axes):
    count = lax.axis_size("row")
    chips = count // 2
    mate_pairs = [(i, i ^ 1) for i in range(count)]
    mates = lax.ppermute(jnp.stack(kernels), "row", mate_pairs)
    wholes = []
    previous = None
    for index, (shard, swap_axis) in enumerate(zip(kernels, swap_axes)):
        if swap_axis is None:
            mine = shard
        else:
            depth = shard.shape[2]
            halves = shard.reshape(shard.shape[:2] + (2, depth // 2) + shard.shape[3:])
            parity = lax.axis_index(swap_axis) % 2
            mine = lax.dynamic_index_in_dim(halves, parity, axis=2, keepdims=False)
        held = [shard, mates[index]]
        for step in range(1, chips):
            if previous is not None:
                mine, _ = lax.optimization_barrier((mine, previous))
            pairs = [(((i // 2 + step) % chips) * 2 + i % 2, i) for i in range(count)]
            fetched = lax.ppermute(mine, "row", pairs)
            previous = fetched
            relayed = lax.ppermute(fetched, "row", mate_pairs)
            if swap_axis is None:
                held += [fetched, relayed]
            else:
                swap_pairs = [(i, i ^ 1) for i in range(lax.axis_size(swap_axis))]
                other = lax.ppermute(fetched, swap_axis, swap_pairs)
                other_relayed = lax.ppermute(other, "row", mate_pairs)
                held += [
                    jnp.concatenate([fetched, other], axis=2),
                    jnp.concatenate([relayed, other_relayed], axis=2),
                ]
        wholes.append(jnp.concatenate(held, axis=2))
    return wholes


def relative_order(channels, swap_axis):
    count = lax.axis_size("row")
    chips = count // 2
    depth = channels // count
    me = lax.axis_index("row")
    chip = me // 2
    core = me % 2
    position = jnp.arange(channels, dtype=jnp.int32)
    block = position // depth
    within = position % depth
    source = 2 * ((chip + block // 2) % chips) + jnp.where(block % 2 == 0, core, 1 - core)
    if swap_axis is None:
        return source * depth + within
    half = depth // 2
    parity = lax.axis_index(swap_axis) % 2
    shuffled = (parity ^ (within // half)) * half + within % half
    return source * depth + jnp.where(block >= 2, shuffled, within)


def to_relative(activation, order):
    natural = jnp.arange(activation.shape[-1], dtype=jnp.int32)[:, None]
    chooser = (natural == order[None, :]).astype(activation.dtype)
    moved = jnp.dot(activation, chooser, preferred_element_type=jnp.float32)
    return moved.astype(activation.dtype)


def conv_relative(activation, kernel, order):
    return conv_valid(to_relative(activation, order), kernel)


def conv_valid(activation, kernel):
    return lax.conv_general_dilated(
        activation,
        kernel,
        window_strides=(1, 1),
        padding="VALID",
        dimension_numbers=("NHWC", "HWIO", "NHWC"),
        preferred_element_type=jnp.float32,
    )


def body(
    latent_in,
    cached_mid,
    cached_out,
    edit_tiles,
    norm1_mean,
    norm1_rstd,
    norm1_gain,
    norm1_shift,
    conv1_weight,
    conv1_bias,
    step_embed,
    norm2_mean,
    norm2_rstd,
    norm2_gain,
    norm2_shift,
    conv2_weight,
    conv2_bias,
):
    requests, rows_dev, cols_dev, channels = latent_in.shape
    tiles_down = rows_dev // TILE
    tiles_across = cols_dev // TILE
    rows_total = rows_dev * lax.axis_size("row")
    cols_total = cols_dev * lax.axis_size("col")
    tile_cols_total = tiles_across * lax.axis_size("col")
    groups_total = norm1_mean.shape[1]
    per_group = channels // groups_total

    first_whole, second_whole = gather_weights([conv1_weight, conv2_weight], (None, "groups"))
    first_order = relative_order(channels, None)
    order = relative_order(channels, "groups")

    def expand(values):
        return jnp.repeat(values, per_group, axis=1)[:, None, None, :]

    stacked = jnp.stack([latent_in, cached_mid])
    padded = padded_2(stacked, (("row", 2), ("col", 3)), 1)
    inputs_pad = padded[0].astype(jnp.float32)
    margins_pad = padded[1].astype(jnp.float32)

    row_start = lax.axis_index("row") * rows_dev - 1
    col_start = lax.axis_index("col") * cols_dev - 1
    cell_rows = row_start + jnp.arange(rows_dev + 2, dtype=jnp.int32)
    cell_cols = col_start + jnp.arange(cols_dev + 2, dtype=jnp.int32)
    inside = ((cell_rows >= 0) & (cell_rows < rows_total))[:, None] & (
        (cell_cols >= 0) & (cell_cols < cols_total)
    )[None, :]
    inside = inside.astype(jnp.float32)[None, :, :, None]

    first_act = (
        jax.nn.silu(
            (inputs_pad - expand(norm1_mean)) * expand(norm1_rstd) * norm1_gain + norm1_shift
        )
        * inside
    ).astype(jnp.bfloat16)
    fresh_mid = (
        conv_relative(first_act, first_whole, first_order) + conv1_bias + step_embed[:, None, None, :]
    )

    if tiles_down != 1:
        raise ValueError("tiles_down")
    second_mean = expand(norm2_mean)
    second_rstd = expand(norm2_rstd)

    def second_norm(values):
        return jax.nn.silu((values - second_mean) * second_rstd * norm2_gain + norm2_shift)

    cached_act = to_relative((second_norm(margins_pad) * inside).astype(jnp.bfloat16), order)
    fresh_act = to_relative(second_norm(fresh_mid).astype(jnp.bfloat16), order)
    blended = lax.dynamic_update_slice(cached_act, fresh_act, (0, 1, 1, 0))
    second_sum = conv_valid(blended, second_whole)
    fixes = jnp.zeros_like(second_sum)
    for boundary in range(1, tiles_across):
        edge_col = boundary * TILE
        for out_col, in_col, tap in ((edge_col - 1, edge_col + 1, 2), (edge_col, edge_col, 0)):
            pair = jnp.concatenate(
                [cached_act[:, :, in_col : in_col + 1], blended[:, :, in_col : in_col + 1]]
            )
            moved = conv_valid(pair, second_whole[:, tap : tap + 1])
            change = moved[:requests] - moved[requests:]
            fixes = fixes + jnp.pad(
                change, ((0, 0), (0, 0), (out_col, cols_dev - out_col - 1), (0, 0))
            )
    second_sum = second_sum + fixes
    renewed = (
        second_sum + conv2_bias + inputs_pad[:, 1 : 1 + rows_dev, 1 : 1 + cols_dev]
    ).astype(jnp.bfloat16)

    own_rows = lax.axis_index("row") * tiles_down + jnp.arange(tiles_down, dtype=jnp.int32)
    own_cols = lax.axis_index("col") * tiles_across + jnp.arange(tiles_across, dtype=jnp.int32)
    tile_numbers = own_rows[:, None] * tile_cols_total + own_cols[None, :]
    edited = jnp.any(edit_tiles[:, None, None, :] == tile_numbers[None, :, :, None], axis=-1)
    cell_mask = jnp.repeat(jnp.repeat(edited, TILE, axis=1), TILE, axis=2)
    return jnp.where(cell_mask[..., None], renewed, cached_out)


def solution(mesh):
    placed = (
        P("groups", "row", "col", None),
        P("groups", "row", "col", None),
        P("groups", "row", "col", None),
        P("groups", None),
        P("groups", None),
        P("groups", None),
        P(),
        P(),
        P(None, None, "row", None),
        P(),
        P("groups", None),
        P("groups", None),
        P("groups", None),
        P(),
        P(),
        P(None, None, "row", None),
        P(),
    )
    return jax.shard_map(
        body, mesh=mesh, in_specs=placed, out_specs=P("groups", "row", "col", None), check_vma=False
    )
```

```python
import jax
import jax.numpy as jnp
from jax import lax
from jax.sharding import PartitionSpec as P

TILE = 4


def padded_2(block, sides, width):
    for axis, dim in sides:
        count = lax.axis_size(axis)
        forward = [(i, i + 1) for i in range(count - 1)]
        backward = [(target, source) for source, target in forward]
        low = lax.ppermute(
            lax.slice_in_dim(block, block.shape[dim] - width, None, axis=dim), axis, forward
        )
        high = lax.ppermute(lax.slice_in_dim(block, 0, width, axis=dim), axis, backward)
        block = jnp.concatenate([low, block, high], axis=dim)
    return block


def gather_weights(kernels, swap_axes):
    count = lax.axis_size("row")
    chips = count // 2
    mate_pairs = [(i, i ^ 1) for i in range(count)]
    wholes = []
    previous = None
    for shard, swap_axis in zip(kernels, swap_axes):
        swap_pairs = [(i, i ^ 1) for i in range(lax.axis_size(swap_axis))]
        parity = lax.axis_index(swap_axis) % 2
        depth = shard.shape[2]
        halves = shard.reshape(shard.shape[:2] + (2, depth // 2) + shard.shape[3:])
        mine = lax.dynamic_index_in_dim(halves, parity, axis=2, keepdims=False)
        held = [shard, lax.ppermute(shard, "row", mate_pairs)]
        for step in range(1, chips):
            if previous is not None:
                mine, _ = lax.optimization_barrier((mine, previous))
            pairs = [(((i // 2 + step) % chips) * 2 + i % 2, i) for i in range(count)]
            fetched = lax.ppermute(mine, "row", pairs)
            other = lax.ppermute(fetched, swap_axis, swap_pairs)
            previous = other
            relayed = lax.ppermute(fetched, "row", mate_pairs)
            other_relayed = lax.ppermute(other, "row", mate_pairs)
            held += [
                jnp.concatenate([fetched, other], axis=2),
                jnp.concatenate([relayed, other_relayed], axis=2),
            ]
        wholes.append(jnp.concatenate(held, axis=2))
    return wholes


def relative_order(channels, swap_axis):
    count = lax.axis_size("row")
    chips = count // 2
    depth = channels // count
    me = lax.axis_index("row")
    chip = me // 2
    core = me % 2
    position = jnp.arange(channels, dtype=jnp.int32)
    block = position // depth
    within = position % depth
    source = 2 * ((chip + block // 2) % chips) + jnp.where(block % 2 == 0, core, 1 - core)
    half = depth // 2
    parity = lax.axis_index(swap_axis) % 2
    shuffled = (parity ^ (within // half)) * half + within % half
    return source * depth + jnp.where(block >= 2, shuffled, within)


def to_relative(activation, order):
    natural = jnp.arange(activation.shape[-1], dtype=jnp.int32)[:, None]
    chooser = (natural == order[None, :]).astype(activation.dtype)
    moved = jnp.dot(activation, chooser, preferred_element_type=jnp.float32)
    return moved.astype(activation.dtype)


def conv_relative(activation, kernel, order):
    return conv_valid(to_relative(activation, order), kernel)


def conv_valid(activation, kernel):
    return lax.conv_general_dilated(
        activation,
        kernel,
        window_strides=(1, 1),
        padding="VALID",
        dimension_numbers=("NHWC", "HWIO", "NHWC"),
        preferred_element_type=jnp.float32,
    )


def body(
    latent_in,
    cached_mid,
    cached_out,
    edit_tiles,
    norm1_mean,
    norm1_rstd,
    norm1_gain,
    norm1_shift,
    conv1_weight,
    conv1_bias,
    step_embed,
    norm2_mean,
    norm2_rstd,
    norm2_gain,
    norm2_shift,
    conv2_weight,
    conv2_bias,
):
    requests, rows_dev, cols_dev, channels = latent_in.shape
    tiles_down = rows_dev // TILE
    tiles_across = cols_dev // TILE
    rows_total = rows_dev * lax.axis_size("row")
    cols_total = cols_dev * lax.axis_size("col")
    tile_cols_total = tiles_across * lax.axis_size("col")
    groups_total = norm1_mean.shape[1]
    per_group = channels // groups_total

    first_whole, second_whole = gather_weights([conv1_weight, conv2_weight], ("groups", "col"))
    first_order = relative_order(channels, "groups")
    order = relative_order(channels, "col")

    def expand(values):
        return jnp.repeat(values, per_group, axis=1)[:, None, None, :]

    stacked = jnp.stack([latent_in, cached_mid])
    padded = padded_2(stacked, (("row", 2), ("col", 3)), 1)
    inputs_pad = padded[0].astype(jnp.float32)
    margins_pad = padded[1].astype(jnp.float32)

    row_start = lax.axis_index("row") * rows_dev - 1
    col_start = lax.axis_index("col") * cols_dev - 1
    cell_rows = row_start + jnp.arange(rows_dev + 2, dtype=jnp.int32)
    cell_cols = col_start + jnp.arange(cols_dev + 2, dtype=jnp.int32)
    inside = ((cell_rows >= 0) & (cell_rows < rows_total))[:, None] & (
        (cell_cols >= 0) & (cell_cols < cols_total)
    )[None, :]
    inside = inside.astype(jnp.float32)[None, :, :, None]

    first_act = (
        jax.nn.silu(
            (inputs_pad - expand(norm1_mean)) * expand(norm1_rstd) * norm1_gain + norm1_shift
        )
        * inside
    ).astype(jnp.bfloat16)
    fresh_mid = (
        conv_relative(first_act, first_whole, first_order) + conv1_bias + step_embed[:, None, None, :]
    )

    if tiles_down != 1:
        raise ValueError("tiles_down")
    second_mean = expand(norm2_mean)
    second_rstd = expand(norm2_rstd)

    def second_norm(values):
        return jax.nn.silu((values - second_mean) * second_rstd * norm2_gain + norm2_shift)

    cached_act = to_relative((second_norm(margins_pad) * inside).astype(jnp.bfloat16), order)
    fresh_act = to_relative(second_norm(fresh_mid).astype(jnp.bfloat16), order)
    blended = lax.dynamic_update_slice(cached_act, fresh_act, (0, 1, 1, 0))
    second_sum = conv_valid(blended, second_whole)
    fixes = jnp.zeros_like(second_sum)
    for boundary in range(1, tiles_across):
        edge_col = boundary * TILE
        for out_col, in_col, tap in ((edge_col - 1, edge_col + 1, 2), (edge_col, edge_col, 0)):
            pair = jnp.concatenate(
                [cached_act[:, :, in_col : in_col + 1], blended[:, :, in_col : in_col + 1]]
            )
            moved = conv_valid(pair, second_whole[:, tap : tap + 1])
            change = moved[:requests] - moved[requests:]
            fixes = fixes + jnp.pad(
                change, ((0, 0), (0, 0), (out_col, cols_dev - out_col - 1), (0, 0))
            )
    second_sum = second_sum + fixes
    renewed = (
        second_sum + conv2_bias + inputs_pad[:, 1 : 1 + rows_dev, 1 : 1 + cols_dev]
    ).astype(jnp.bfloat16)

    own_rows = lax.axis_index("row") * tiles_down + jnp.arange(tiles_down, dtype=jnp.int32)
    own_cols = lax.axis_index("col") * tiles_across + jnp.arange(tiles_across, dtype=jnp.int32)
    tile_numbers = own_rows[:, None] * tile_cols_total + own_cols[None, :]
    edited = jnp.any(edit_tiles[:, None, None, :] == tile_numbers[None, :, :, None], axis=-1)
    cell_mask = jnp.repeat(jnp.repeat(edited, TILE, axis=1), TILE, axis=2)
    return jnp.where(cell_mask[..., None], renewed, cached_out)


def solution(mesh):
    placed = (
        P("groups", "row", "col", None),
        P("groups", "row", "col", None),
        P("groups", "row", "col", None),
        P("groups", None),
        P("groups", None),
        P("groups", None),
        P(),
        P(),
        P(None, None, "row", None),
        P(),
        P("groups", None),
        P("groups", None),
        P("groups", None),
        P(),
        P(),
        P(None, None, "row", None),
        P(),
    )
    return jax.shard_map(
        body, mesh=mesh, in_specs=placed, out_specs=P("groups", "row", "col", None), check_vma=False
    )
```

```python
import jax
import jax.numpy as jnp
from jax import lax
from jax.sharding import PartitionSpec as P

TILE = 4


def padded_2(block, sides, width):
    for axis, dim in sides:
        count = lax.axis_size(axis)
        forward = [(i, i + 1) for i in range(count - 1)]
        backward = [(target, source) for source, target in forward]
        low = lax.ppermute(
            lax.slice_in_dim(block, block.shape[dim] - width, None, axis=dim), axis, forward
        )
        high = lax.ppermute(lax.slice_in_dim(block, 0, width, axis=dim), axis, backward)
        block = jnp.concatenate([low, block, high], axis=dim)
    return block


def gather_weights(kernels):
    count = lax.axis_size("row")
    chips = count // 2
    y_pairs = [(i, i ^ 1) for i in range(lax.axis_size("groups"))]
    mate_pairs = [(i, i ^ 1) for i in range(count)]
    parity = lax.axis_index("groups") % 2
    wholes = []
    previous = None
    for shard in kernels:
        depth = shard.shape[2]
        halves = shard.reshape(shard.shape[:2] + (2, depth // 2) + shard.shape[3:])
        mine = lax.dynamic_index_in_dim(halves, parity, axis=2, keepdims=False)
        held = [shard, lax.ppermute(shard, "row", mate_pairs)]
        for step in range(1, chips):
            if previous is not None:
                mine, _ = lax.optimization_barrier((mine, previous))
            pairs = [(((i // 2 + step) % chips) * 2 + i % 2, i) for i in range(count)]
            fetched = lax.ppermute(mine, "row", pairs)
            previous = fetched
            other = lax.ppermute(fetched, "groups", y_pairs)
            relayed = lax.ppermute(fetched, "row", mate_pairs)
            other_relayed = lax.ppermute(other, "row", mate_pairs)
            held += [
                jnp.concatenate([fetched, other], axis=2),
                jnp.concatenate([relayed, other_relayed], axis=2),
            ]
        wholes.append(jnp.concatenate(held, axis=2))
    return wholes


def relative_order(channels):
    count = lax.axis_size("row")
    chips = count // 2
    depth = channels // count
    me = lax.axis_index("row")
    chip = me // 2
    core = me % 2
    position = jnp.arange(channels, dtype=jnp.int32)
    block = position // depth
    within = position % depth
    source = 2 * ((chip + block // 2) % chips) + jnp.where(block % 2 == 0, core, 1 - core)
    half = depth // 2
    parity = lax.axis_index("groups") % 2
    shuffled = (parity ^ (within // half)) * half + within % half
    return source * depth + jnp.where(block >= 2, shuffled, within)


def to_relative(activation, order):
    natural = jnp.arange(activation.shape[-1], dtype=jnp.int32)[:, None]
    chooser = (natural == order[None, :]).astype(activation.dtype)
    moved = jnp.dot(activation, chooser, preferred_element_type=jnp.float32)
    return moved.astype(activation.dtype)


def conv_relative(activation, kernel, order):
    return conv_valid(to_relative(activation, order), kernel)


def conv_valid(activation, kernel):
    return lax.conv_general_dilated(
        activation,
        kernel,
        window_strides=(1, 1),
        padding="VALID",
        dimension_numbers=("NHWC", "HWIO", "NHWC"),
        preferred_element_type=jnp.float32,
    )


def body(
    latent_in,
    cached_mid,
    cached_out,
    edit_tiles,
    norm1_mean,
    norm1_rstd,
    norm1_gain,
    norm1_shift,
    conv1_weight,
    conv1_bias,
    step_embed,
    norm2_mean,
    norm2_rstd,
    norm2_gain,
    norm2_shift,
    conv2_weight,
    conv2_bias,
):
    requests, rows_dev, cols_dev, channels = latent_in.shape
    tiles_down = rows_dev // TILE
    tiles_across = cols_dev // TILE
    rows_total = rows_dev * lax.axis_size("row")
    cols_total = cols_dev * lax.axis_size("col")
    tile_cols_total = tiles_across * lax.axis_size("col")
    groups_total = norm1_mean.shape[1]
    per_group = channels // groups_total

    first_whole, second_whole = gather_weights([conv1_weight, conv2_weight])
    order = relative_order(channels)

    def expand(values):
        return jnp.repeat(values, per_group, axis=1)[:, None, None, :]

    stacked = jnp.stack([latent_in, cached_mid])
    padded = padded_2(stacked, (("row", 2), ("col", 3)), 1)
    inputs_pad = padded[0].astype(jnp.float32)
    margins_pad = padded[1].astype(jnp.float32)

    row_start = lax.axis_index("row") * rows_dev - 1
    col_start = lax.axis_index("col") * cols_dev - 1
    cell_rows = row_start + jnp.arange(rows_dev + 2, dtype=jnp.int32)
    cell_cols = col_start + jnp.arange(cols_dev + 2, dtype=jnp.int32)
    inside = ((cell_rows >= 0) & (cell_rows < rows_total))[:, None] & (
        (cell_cols >= 0) & (cell_cols < cols_total)
    )[None, :]
    inside = inside.astype(jnp.float32)[None, :, :, None]

    first_act = (
        jax.nn.silu(
            (inputs_pad - expand(norm1_mean)) * expand(norm1_rstd) * norm1_gain + norm1_shift
        )
        * inside
    ).astype(jnp.bfloat16)
    fresh_mid = (
        conv_relative(first_act, first_whole, order) + conv1_bias + step_embed[:, None, None, :]
    )

    if tiles_down != 1:
        raise ValueError("tiles_down")
    second_mean = expand(norm2_mean)
    second_rstd = expand(norm2_rstd)

    def second_norm(values):
        return jax.nn.silu((values - second_mean) * second_rstd * norm2_gain + norm2_shift)

    cached_act = to_relative((second_norm(margins_pad) * inside).astype(jnp.bfloat16), order)
    fresh_act = to_relative(second_norm(fresh_mid).astype(jnp.bfloat16), order)
    blended = lax.dynamic_update_slice(cached_act, fresh_act, (0, 1, 1, 0))
    second_sum = conv_valid(blended, second_whole)
    fixes = jnp.zeros_like(second_sum)
    for boundary in range(1, tiles_across):
        edge_col = boundary * TILE
        for out_col, in_col, tap in ((edge_col - 1, edge_col + 1, 2), (edge_col, edge_col, 0)):
            pair = jnp.stack([cached_act[:, :, in_col], blended[:, :, in_col]])
            moved = None
            for tap_row in range(3):
                term = jnp.dot(
                    pair[:, :, tap_row : tap_row + rows_dev],
                    second_whole[tap_row, tap],
                    preferred_element_type=jnp.float32,
                )
                moved = term if moved is None else moved + term
            change = (moved[0] - moved[1])[:, :, None, :]
            fixes = fixes + jnp.pad(
                change, ((0, 0), (0, 0), (out_col, cols_dev - out_col - 1), (0, 0))
            )
    second_sum = second_sum + fixes
    renewed = (
        second_sum + conv2_bias + inputs_pad[:, 1 : 1 + rows_dev, 1 : 1 + cols_dev]
    ).astype(jnp.bfloat16)

    own_rows = lax.axis_index("row") * tiles_down + jnp.arange(tiles_down, dtype=jnp.int32)
    own_cols = lax.axis_index("col") * tiles_across + jnp.arange(tiles_across, dtype=jnp.int32)
    tile_numbers = own_rows[:, None] * tile_cols_total + own_cols[None, :]
    edited = jnp.any(edit_tiles[:, None, None, :] == tile_numbers[None, :, :, None], axis=-1)
    cell_mask = jnp.repeat(jnp.repeat(edited, TILE, axis=1), TILE, axis=2)
    return jnp.where(cell_mask[..., None], renewed, cached_out)


def solution(mesh):
    placed = (
        P("groups", "row", "col", None),
        P("groups", "row", "col", None),
        P("groups", "row", "col", None),
        P("groups", None),
        P("groups", None),
        P("groups", None),
        P(),
        P(),
        P(None, None, "row", None),
        P(),
        P("groups", None),
        P("groups", None),
        P("groups", None),
        P(),
        P(),
        P(None, None, "row", None),
        P(),
    )
    return jax.shard_map(
        body, mesh=mesh, in_specs=placed, out_specs=P("groups", "row", "col", None), check_vma=False
    )
```

```python
import jax
import jax.numpy as jnp
from jax import lax
from jax.sharding import PartitionSpec as P

TILE = 4


def padded_2(block, sides, width):
    for axis, dim in sides:
        count = lax.axis_size(axis)
        forward = [(i, i + 1) for i in range(count - 1)]
        backward = [(target, source) for source, target in forward]
        low = lax.ppermute(
            lax.slice_in_dim(block, block.shape[dim] - width, None, axis=dim), axis, forward
        )
        high = lax.ppermute(lax.slice_in_dim(block, 0, width, axis=dim), axis, backward)
        block = jnp.concatenate([low, block, high], axis=dim)
    return block


def gather_weights(kernels):
    count = lax.axis_size("row")
    chips = count // 2
    mate_pairs = [(i, i ^ 1) for i in range(count)]
    parity = lax.axis_index("groups")
    wholes = []
    previous = None
    for shard in kernels:
        depth = shard.shape[2]
        halves = shard.reshape(shard.shape[:2] + (2, depth // 2) + shard.shape[3:])
        mine = lax.dynamic_index_in_dim(halves, parity, axis=2, keepdims=False)
        held = [shard, lax.ppermute(shard, "row", mate_pairs)]
        for step in range(1, chips):
            if previous is not None:
                mine, _ = lax.optimization_barrier((mine, previous))
            pairs = [(((i // 2 + step) % chips) * 2 + i % 2, i) for i in range(count)]
            fetched = lax.ppermute(mine, "row", pairs)
            previous = fetched
            rebuilt = lax.all_gather(fetched, "groups", axis=2, tiled=True)
            held += [rebuilt, lax.ppermute(rebuilt, "row", mate_pairs)]
        wholes.append(jnp.concatenate(held, axis=2))
    return wholes


def relative_order(channels):
    count = lax.axis_size("row")
    chips = count // 2
    depth = channels // count
    me = lax.axis_index("row")
    chip = me // 2
    core = me % 2
    position = jnp.arange(channels, dtype=jnp.int32)
    block = position // depth
    within = position % depth
    source = 2 * ((chip + block // 2) % chips) + jnp.where(block % 2 == 0, core, 1 - core)
    return source * depth + within


def to_relative(activation, order):
    natural = jnp.arange(activation.shape[-1], dtype=jnp.int32)[:, None]
    chooser = (natural == order[None, :]).astype(activation.dtype)
    moved = jnp.dot(activation, chooser, preferred_element_type=jnp.float32)
    return moved.astype(activation.dtype)


def conv_relative(activation, kernel, order):
    return conv_valid(to_relative(activation, order), kernel)


def conv_valid(activation, kernel):
    return lax.conv_general_dilated(
        activation,
        kernel,
        window_strides=(1, 1),
        padding="VALID",
        dimension_numbers=("NHWC", "HWIO", "NHWC"),
        preferred_element_type=jnp.float32,
    )


def body(
    latent_in,
    cached_mid,
    cached_out,
    edit_tiles,
    norm1_mean,
    norm1_rstd,
    norm1_gain,
    norm1_shift,
    conv1_weight,
    conv1_bias,
    step_embed,
    norm2_mean,
    norm2_rstd,
    norm2_gain,
    norm2_shift,
    conv2_weight,
    conv2_bias,
):
    requests, rows_dev, cols_dev, channels = latent_in.shape
    tiles_down = rows_dev // TILE
    tiles_across = cols_dev // TILE
    rows_total = rows_dev * lax.axis_size("row")
    cols_total = cols_dev * lax.axis_size("col")
    tile_cols_total = tiles_across * lax.axis_size("col")
    groups_total = norm1_mean.shape[1]
    per_group = channels // groups_total

    first_whole, second_whole = gather_weights([conv1_weight, conv2_weight])
    order = relative_order(channels)

    def expand(values):
        return jnp.repeat(values, per_group, axis=1)[:, None, None, :]

    stacked = jnp.stack([latent_in, cached_mid])
    padded = padded_2(stacked, (("row", 2), ("col", 3)), 1)
    inputs_pad = padded[0].astype(jnp.float32)
    margins_pad = padded[1].astype(jnp.float32)

    row_start = lax.axis_index("row") * rows_dev - 1
    col_start = lax.axis_index("col") * cols_dev - 1
    cell_rows = row_start + jnp.arange(rows_dev + 2, dtype=jnp.int32)
    cell_cols = col_start + jnp.arange(cols_dev + 2, dtype=jnp.int32)
    inside = ((cell_rows >= 0) & (cell_rows < rows_total))[:, None] & (
        (cell_cols >= 0) & (cell_cols < cols_total)
    )[None, :]
    inside = inside.astype(jnp.float32)[None, :, :, None]

    first_act = (
        jax.nn.silu(
            (inputs_pad - expand(norm1_mean)) * expand(norm1_rstd) * norm1_gain + norm1_shift
        )
        * inside
    ).astype(jnp.bfloat16)
    fresh_mid = (
        conv_relative(first_act, first_whole, order) + conv1_bias + step_embed[:, None, None, :]
    )

    if tiles_down != 1:
        raise ValueError("tiles_down")
    second_mean = expand(norm2_mean)
    second_rstd = expand(norm2_rstd)

    def second_norm(values):
        return jax.nn.silu((values - second_mean) * second_rstd * norm2_gain + norm2_shift)

    cached_act = to_relative((second_norm(margins_pad) * inside).astype(jnp.bfloat16), order)
    fresh_act = to_relative(second_norm(fresh_mid).astype(jnp.bfloat16), order)
    blended = lax.dynamic_update_slice(cached_act, fresh_act, (0, 1, 1, 0))
    second_sum = conv_valid(blended, second_whole)
    fixes = jnp.zeros_like(second_sum)
    for boundary in range(1, tiles_across):
        edge_col = boundary * TILE
        for out_col, in_col, tap in ((edge_col - 1, edge_col + 1, 2), (edge_col, edge_col, 0)):
            pair = jnp.concatenate(
                [cached_act[:, :, in_col : in_col + 1], blended[:, :, in_col : in_col + 1]]
            )
            moved = conv_valid(pair, second_whole[:, tap : tap + 1])
            change = moved[:requests] - moved[requests:]
            fixes = fixes + jnp.pad(
                change, ((0, 0), (0, 0), (out_col, cols_dev - out_col - 1), (0, 0))
            )
    second_sum = second_sum + fixes
    renewed = (
        second_sum + conv2_bias + inputs_pad[:, 1 : 1 + rows_dev, 1 : 1 + cols_dev]
    ).astype(jnp.bfloat16)

    own_rows = lax.axis_index("row") * tiles_down + jnp.arange(tiles_down, dtype=jnp.int32)
    own_cols = lax.axis_index("col") * tiles_across + jnp.arange(tiles_across, dtype=jnp.int32)
    tile_numbers = own_rows[:, None] * tile_cols_total + own_cols[None, :]
    edited = jnp.any(edit_tiles[:, None, None, :] == tile_numbers[None, :, :, None], axis=-1)
    cell_mask = jnp.repeat(jnp.repeat(edited, TILE, axis=1), TILE, axis=2)
    return jnp.where(cell_mask[..., None], renewed, cached_out)


def solution(mesh):
    placed = (
        P("groups", "row", "col", None),
        P("groups", "row", "col", None),
        P("groups", "row", "col", None),
        P("groups", None),
        P("groups", None),
        P("groups", None),
        P(),
        P(),
        P(None, None, "row", None),
        P(),
        P("groups", None),
        P("groups", None),
        P("groups", None),
        P(),
        P(),
        P(None, None, "row", None),
        P(),
    )
    return jax.shard_map(
        body, mesh=mesh, in_specs=placed, out_specs=P("groups", "row", "col", None), check_vma=False
    )
```

```python
import jax
import jax.numpy as jnp
from jax import lax
from jax.sharding import PartitionSpec as P

TILE = 4


def padded_2(block, sides, width):
    for axis, dim in sides:
        count = lax.axis_size(axis)
        forward = [(i, i + 1) for i in range(count - 1)]
        backward = [(target, source) for source, target in forward]
        low = lax.ppermute(
            lax.slice_in_dim(block, block.shape[dim] - width, None, axis=dim), axis, forward
        )
        high = lax.ppermute(lax.slice_in_dim(block, 0, width, axis=dim), axis, backward)
        block = jnp.concatenate([low, block, high], axis=dim)
    return block


def gather_weights(kernels):
    count = lax.axis_size("row")
    chips = count // 2
    y_pairs = [(i, i ^ 1) for i in range(lax.axis_size("groups"))]
    mate_pairs = [(i, i ^ 1) for i in range(count)]
    parity = lax.axis_index("groups") % 2
    wholes = []
    previous = None
    for shard in kernels:
        depth = shard.shape[2]
        halves = shard.reshape(shard.shape[:2] + (2, depth // 2) + shard.shape[3:])
        mine = lax.dynamic_index_in_dim(halves, parity, axis=2, keepdims=False)
        held = [shard, lax.ppermute(shard, "row", mate_pairs)]
        for step in range(1, chips):
            if previous is not None:
                mine, _ = lax.optimization_barrier((mine, previous))
            pairs = [(((i // 2 + step) % chips) * 2 + i % 2, i) for i in range(count)]
            fetched = lax.ppermute(mine, "row", pairs)
            previous = fetched
            other = lax.ppermute(fetched, "groups", y_pairs)
            relayed = lax.ppermute(fetched, "row", mate_pairs)
            other_relayed = lax.ppermute(other, "row", mate_pairs)
            held += [
                jnp.concatenate([fetched, other], axis=2),
                jnp.concatenate([relayed, other_relayed], axis=2),
            ]
        wholes.append(jnp.concatenate(held, axis=2))
    return wholes


def relative_order(channels):
    count = lax.axis_size("row")
    chips = count // 2
    depth = channels // count
    me = lax.axis_index("row")
    chip = me // 2
    core = me % 2
    position = jnp.arange(channels, dtype=jnp.int32)
    block = position // depth
    within = position % depth
    source = 2 * ((chip + block // 2) % chips) + jnp.where(block % 2 == 0, core, 1 - core)
    half = depth // 2
    parity = lax.axis_index("groups") % 2
    shuffled = (parity ^ (within // half)) * half + within % half
    return source * depth + jnp.where(block >= 2, shuffled, within)


def to_relative(activation, order):
    natural = jnp.arange(activation.shape[-1], dtype=jnp.int32)[:, None]
    chooser = (natural == order[None, :]).astype(activation.dtype)
    moved = jnp.dot(activation, chooser, preferred_element_type=jnp.float32)
    return moved.astype(activation.dtype)


def conv_relative(activation, kernel, order):
    return conv_valid(to_relative(activation, order), kernel)


def conv_valid(activation, kernel):
    return lax.conv_general_dilated(
        activation,
        kernel,
        window_strides=(1, 1),
        padding="VALID",
        dimension_numbers=("NHWC", "HWIO", "NHWC"),
        preferred_element_type=jnp.float32,
    )


def body(
    latent_in,
    cached_mid,
    cached_out,
    edit_tiles,
    norm1_mean,
    norm1_rstd,
    norm1_gain,
    norm1_shift,
    conv1_weight,
    conv1_bias,
    step_embed,
    norm2_mean,
    norm2_rstd,
    norm2_gain,
    norm2_shift,
    conv2_weight,
    conv2_bias,
):
    requests, rows_dev, cols_dev, channels = latent_in.shape
    tiles_down = rows_dev // TILE
    tiles_across = cols_dev // TILE
    rows_total = rows_dev * lax.axis_size("row")
    cols_total = cols_dev * lax.axis_size("col")
    tile_cols_total = tiles_across * lax.axis_size("col")
    groups_total = norm1_mean.shape[1]
    per_group = channels // groups_total

    first_whole, second_whole = gather_weights([conv1_weight, conv2_weight])
    order = relative_order(channels)

    def expand(values):
        return jnp.repeat(values, per_group, axis=1)[:, None, None, :]

    stacked = jnp.stack([latent_in, cached_mid])
    padded = padded_2(stacked, (("row", 2), ("col", 3)), 1)
    inputs_pad = padded[0].astype(jnp.float32)
    margins_pad = padded[1].astype(jnp.float32)

    row_start = lax.axis_index("row") * rows_dev - 1
    col_start = lax.axis_index("col") * cols_dev - 1
    cell_rows = row_start + jnp.arange(rows_dev + 2, dtype=jnp.int32)
    cell_cols = col_start + jnp.arange(cols_dev + 2, dtype=jnp.int32)
    inside = ((cell_rows >= 0) & (cell_rows < rows_total))[:, None] & (
        (cell_cols >= 0) & (cell_cols < cols_total)
    )[None, :]
    inside = inside.astype(jnp.float32)[None, :, :, None]

    first_act = (
        jax.nn.silu(
            (inputs_pad - expand(norm1_mean)) * expand(norm1_rstd) * norm1_gain + norm1_shift
        )
        * inside
    ).astype(jnp.bfloat16)
    fresh_mid = (
        conv_relative(first_act, first_whole, order) + conv1_bias + step_embed[:, None, None, :]
    )

    if tiles_down != 1:
        raise ValueError("tiles_down")
    second_mean = expand(norm2_mean)
    second_rstd = expand(norm2_rstd)

    def second_norm(values):
        return jax.nn.silu((values - second_mean) * second_rstd * norm2_gain + norm2_shift)

    cached_act = to_relative((second_norm(margins_pad) * inside).astype(jnp.bfloat16), order)
    fresh_act = to_relative(second_norm(fresh_mid).astype(jnp.bfloat16), order)
    fresh_pad = jnp.pad(fresh_act, ((0, 0), (1, 1), (1, 1), (0, 0)))
    edge = jnp.arange(TILE + 2, dtype=jnp.int32)
    interior = ((edge >= 1) & (edge <= TILE))[:, None] & ((edge >= 1) & (edge <= TILE))[None, :]
    interior = interior[None, :, :, None]
    windows = []
    for tile_across in range(tiles_across):
        cut = slice(tile_across * TILE, tile_across * TILE + TILE + 2)
        windows.append(jnp.where(interior, fresh_pad[:, :, cut], cached_act[:, :, cut]))
    wide_sum = conv_valid(jnp.concatenate(windows, axis=2), second_whole)
    stride = TILE + 2
    second_sum = jnp.concatenate(
        [wide_sum[:, :, t * stride : t * stride + TILE] for t in range(tiles_across)], axis=2
    )
    renewed = (
        second_sum + conv2_bias + inputs_pad[:, 1 : 1 + rows_dev, 1 : 1 + cols_dev]
    ).astype(jnp.bfloat16)

    own_rows = lax.axis_index("row") * tiles_down + jnp.arange(tiles_down, dtype=jnp.int32)
    own_cols = lax.axis_index("col") * tiles_across + jnp.arange(tiles_across, dtype=jnp.int32)
    tile_numbers = own_rows[:, None] * tile_cols_total + own_cols[None, :]
    edited = jnp.any(edit_tiles[:, None, None, :] == tile_numbers[None, :, :, None], axis=-1)
    cell_mask = jnp.repeat(jnp.repeat(edited, TILE, axis=1), TILE, axis=2)
    return jnp.where(cell_mask[..., None], renewed, cached_out)


def solution(mesh):
    placed = (
        P("groups", "row", "col", None),
        P("groups", "row", "col", None),
        P("groups", "row", "col", None),
        P("groups", None),
        P("groups", None),
        P("groups", None),
        P(),
        P(),
        P(None, None, "row", None),
        P(),
        P("groups", None),
        P("groups", None),
        P("groups", None),
        P(),
        P(),
        P(None, None, "row", None),
        P(),
    )
    return jax.shard_map(
        body, mesh=mesh, in_specs=placed, out_specs=P("groups", "row", "col", None), check_vma=False
    )
```

```python
import jax
import jax.numpy as jnp
from jax import lax
from jax.sharding import PartitionSpec as P

TILE = 4


def padded_2(block, sides, width):
    for axis, dim in sides:
        count = lax.axis_size(axis)
        forward = [(i, i + 1) for i in range(count - 1)]
        backward = [(target, source) for source, target in forward]
        low = lax.ppermute(
            lax.slice_in_dim(block, block.shape[dim] - width, None, axis=dim), axis, forward
        )
        high = lax.ppermute(lax.slice_in_dim(block, 0, width, axis=dim), axis, backward)
        block = jnp.concatenate([low, block, high], axis=dim)
    return block


def gather_weights(kernels):
    count = lax.axis_size("row")
    chips = count // 2
    y_pairs = [(i, i ^ 1) for i in range(lax.axis_size("groups"))]
    mate_pairs = [(i, i ^ 1) for i in range(count)]
    parity = lax.axis_index("groups") % 2
    wholes = []
    previous = None
    for shard in kernels:
        depth = shard.shape[2]
        halves = shard.reshape(shard.shape[:2] + (2, depth // 2) + shard.shape[3:])
        mine = lax.dynamic_index_in_dim(halves, parity, axis=2, keepdims=False)
        held = [shard, lax.ppermute(shard, "row", mate_pairs)]
        for step in range(1, chips):
            if previous is not None:
                mine, _ = lax.optimization_barrier((mine, previous))
            pairs = [(((i // 2 + step) % chips) * 2 + i % 2, i) for i in range(count)]
            fetched = lax.ppermute(mine, "row", pairs)
            previous = fetched
            other = lax.ppermute(fetched, "groups", y_pairs)
            relayed = lax.ppermute(fetched, "row", mate_pairs)
            other_relayed = lax.ppermute(other, "row", mate_pairs)
            held += [
                jnp.concatenate([fetched, other], axis=2),
                jnp.concatenate([relayed, other_relayed], axis=2),
            ]
        wholes.append(held)
    return wholes


def relative_order(channels):
    count = lax.axis_size("row")
    chips = count // 2
    depth = channels // count
    me = lax.axis_index("row")
    chip = me // 2
    core = me % 2
    position = jnp.arange(channels, dtype=jnp.int32)
    block = position // depth
    within = position % depth
    source = 2 * ((chip + block // 2) % chips) + jnp.where(block % 2 == 0, core, 1 - core)
    half = depth // 2
    parity = lax.axis_index("groups") % 2
    shuffled = (parity ^ (within // half)) * half + within % half
    return source * depth + jnp.where(block >= 2, shuffled, within)


def to_relative(activation, order):
    natural = jnp.arange(activation.shape[-1], dtype=jnp.int32)[:, None]
    chooser = (natural == order[None, :]).astype(activation.dtype)
    moved = jnp.dot(activation, chooser, preferred_element_type=jnp.float32)
    return moved.astype(activation.dtype)


def conv_relative(activation, kernel, order):
    return conv_valid(to_relative(activation, order), kernel)


def conv_valid(activation, kernel):
    return lax.conv_general_dilated(
        activation,
        kernel,
        window_strides=(1, 1),
        padding="VALID",
        dimension_numbers=("NHWC", "HWIO", "NHWC"),
        preferred_element_type=jnp.float32,
    )


def body(
    latent_in,
    cached_mid,
    cached_out,
    edit_tiles,
    norm1_mean,
    norm1_rstd,
    norm1_gain,
    norm1_shift,
    conv1_weight,
    conv1_bias,
    step_embed,
    norm2_mean,
    norm2_rstd,
    norm2_gain,
    norm2_shift,
    conv2_weight,
    conv2_bias,
):
    requests, rows_dev, cols_dev, channels = latent_in.shape
    tiles_down = rows_dev // TILE
    tiles_across = cols_dev // TILE
    rows_total = rows_dev * lax.axis_size("row")
    cols_total = cols_dev * lax.axis_size("col")
    tile_cols_total = tiles_across * lax.axis_size("col")
    groups_total = norm1_mean.shape[1]
    per_group = channels // groups_total

    first_held, second_held = gather_weights([conv1_weight, conv2_weight])
    first_whole = jnp.concatenate(first_held, axis=2)
    second_local = jnp.concatenate(second_held[:2], axis=2)
    second_remote = jnp.concatenate(second_held[2:], axis=2)
    order = relative_order(channels)

    def expand(values):
        return jnp.repeat(values, per_group, axis=1)[:, None, None, :]

    stacked = jnp.stack([latent_in, cached_mid])
    padded = padded_2(stacked, (("row", 2), ("col", 3)), 1)
    inputs_pad = padded[0].astype(jnp.float32)
    margins_pad = padded[1].astype(jnp.float32)

    row_start = lax.axis_index("row") * rows_dev - 1
    col_start = lax.axis_index("col") * cols_dev - 1
    cell_rows = row_start + jnp.arange(rows_dev + 2, dtype=jnp.int32)
    cell_cols = col_start + jnp.arange(cols_dev + 2, dtype=jnp.int32)
    inside = ((cell_rows >= 0) & (cell_rows < rows_total))[:, None] & (
        (cell_cols >= 0) & (cell_cols < cols_total)
    )[None, :]
    inside = inside.astype(jnp.float32)[None, :, :, None]

    first_act = (
        jax.nn.silu(
            (inputs_pad - expand(norm1_mean)) * expand(norm1_rstd) * norm1_gain + norm1_shift
        )
        * inside
    ).astype(jnp.bfloat16)
    fresh_mid = (
        conv_relative(first_act, first_whole, order) + conv1_bias + step_embed[:, None, None, :]
    )

    if tiles_down != 1:
        raise ValueError("tiles_down")
    second_mean = expand(norm2_mean)
    second_rstd = expand(norm2_rstd)

    def second_norm(values):
        return jax.nn.silu((values - second_mean) * second_rstd * norm2_gain + norm2_shift)

    cached_act = to_relative((second_norm(margins_pad) * inside).astype(jnp.bfloat16), order)
    fresh_act = to_relative(second_norm(fresh_mid).astype(jnp.bfloat16), order)
    fresh_pad = jnp.pad(fresh_act, ((0, 0), (1, 1), (1, 1), (0, 0)))
    edge = jnp.arange(TILE + 2, dtype=jnp.int32)
    interior = ((edge >= 1) & (edge <= TILE))[:, None] & ((edge >= 1) & (edge <= TILE))[None, :]
    interior = interior[None, :, :, None]
    windows = []
    for tile_across in range(tiles_across):
        cut = slice(tile_across * TILE, tile_across * TILE + TILE + 2)
        windows.append(jnp.where(interior, fresh_pad[:, :, cut], cached_act[:, :, cut]))
    wide = jnp.concatenate(windows, axis=2)
    split = second_local.shape[2]
    wide_sum = conv_valid(wide[..., :split], second_local) + conv_valid(
        wide[..., split:], second_remote
    )
    stride = TILE + 2
    second_sum = jnp.concatenate(
        [wide_sum[:, :, t * stride : t * stride + TILE] for t in range(tiles_across)], axis=2
    )
    renewed = (
        second_sum + conv2_bias + inputs_pad[:, 1 : 1 + rows_dev, 1 : 1 + cols_dev]
    ).astype(jnp.bfloat16)

    own_rows = lax.axis_index("row") * tiles_down + jnp.arange(tiles_down, dtype=jnp.int32)
    own_cols = lax.axis_index("col") * tiles_across + jnp.arange(tiles_across, dtype=jnp.int32)
    tile_numbers = own_rows[:, None] * tile_cols_total + own_cols[None, :]
    edited = jnp.any(edit_tiles[:, None, None, :] == tile_numbers[None, :, :, None], axis=-1)
    cell_mask = jnp.repeat(jnp.repeat(edited, TILE, axis=1), TILE, axis=2)
    return jnp.where(cell_mask[..., None], renewed, cached_out)


def solution(mesh):
    placed = (
        P("groups", "row", "col", None),
        P("groups", "row", "col", None),
        P("groups", "row", "col", None),
        P("groups", None),
        P("groups", None),
        P("groups", None),
        P(),
        P(),
        P(None, None, "row", None),
        P(),
        P("groups", None),
        P("groups", None),
        P("groups", None),
        P(),
        P(),
        P(None, None, "row", None),
        P(),
    )
    return jax.shard_map(
        body, mesh=mesh, in_specs=placed, out_specs=P("groups", "row", "col", None), check_vma=False
    )
```

```python
import jax
import jax.numpy as jnp
from jax import lax
from jax.sharding import PartitionSpec as P

TILE = 4


def padded_2(block, sides, width):
    for axis, dim in sides:
        count = lax.axis_size(axis)
        forward = [(i, i + 1) for i in range(count - 1)]
        backward = [(target, source) for source, target in forward]
        low = lax.ppermute(
            lax.slice_in_dim(block, block.shape[dim] - width, None, axis=dim), axis, forward
        )
        high = lax.ppermute(lax.slice_in_dim(block, 0, width, axis=dim), axis, backward)
        block = jnp.concatenate([low, block, high], axis=dim)
    return block


def gather_weights(kernels):
    count = lax.axis_size("row")
    chips = count // 2
    y_pairs = [(i, i ^ 1) for i in range(lax.axis_size("groups"))]
    mate_pairs = [(i, i ^ 1) for i in range(count)]
    parity = lax.axis_index("groups") % 2
    wholes = []
    previous = None
    for shard in kernels:
        depth = shard.shape[2]
        halves = shard.reshape(shard.shape[:2] + (2, depth // 2) + shard.shape[3:])
        mine = lax.dynamic_index_in_dim(halves, parity, axis=2, keepdims=False)
        held = [shard, lax.ppermute(shard, "row", mate_pairs)]
        for step in range(1, chips):
            if previous is not None:
                mine, _ = lax.optimization_barrier((mine, previous))
            pairs = [(((i // 2 + step) % chips) * 2 + i % 2, i) for i in range(count)]
            fetched = lax.ppermute(mine, "row", pairs)
            previous = fetched
            other = lax.ppermute(fetched, "groups", y_pairs)
            relayed = lax.ppermute(fetched, "row", mate_pairs)
            other_relayed = lax.ppermute(other, "row", mate_pairs)
            held += [
                jnp.concatenate([fetched, other], axis=2),
                jnp.concatenate([relayed, other_relayed], axis=2),
            ]
        wholes.append(held)
    return wholes


def relative_order(channels):
    count = lax.axis_size("row")
    chips = count // 2
    depth = channels // count
    me = lax.axis_index("row")
    chip = me // 2
    core = me % 2
    position = jnp.arange(channels, dtype=jnp.int32)
    block = position // depth
    within = position % depth
    source = 2 * ((chip + block // 2) % chips) + jnp.where(block % 2 == 0, core, 1 - core)
    half = depth // 2
    parity = lax.axis_index("groups") % 2
    shuffled = (parity ^ (within // half)) * half + within % half
    return source * depth + jnp.where(block >= 2, shuffled, within)


def to_relative(activation, order):
    natural = jnp.arange(activation.shape[-1], dtype=jnp.int32)[:, None]
    chooser = (natural == order[None, :]).astype(activation.dtype)
    moved = jnp.dot(activation, chooser, preferred_element_type=jnp.float32)
    return moved.astype(activation.dtype)


def conv_relative(activation, kernel, order):
    return conv_valid(to_relative(activation, order), kernel)


def conv_valid(activation, kernel):
    return lax.conv_general_dilated(
        activation,
        kernel,
        window_strides=(1, 1),
        padding="VALID",
        dimension_numbers=("NHWC", "HWIO", "NHWC"),
        preferred_element_type=jnp.float32,
    )


def body(
    latent_in,
    cached_mid,
    cached_out,
    edit_tiles,
    norm1_mean,
    norm1_rstd,
    norm1_gain,
    norm1_shift,
    conv1_weight,
    conv1_bias,
    step_embed,
    norm2_mean,
    norm2_rstd,
    norm2_gain,
    norm2_shift,
    conv2_weight,
    conv2_bias,
):
    requests, rows_dev, cols_dev, channels = latent_in.shape
    tiles_down = rows_dev // TILE
    tiles_across = cols_dev // TILE
    rows_total = rows_dev * lax.axis_size("row")
    cols_total = cols_dev * lax.axis_size("col")
    tile_cols_total = tiles_across * lax.axis_size("col")
    groups_total = norm1_mean.shape[1]
    per_group = channels // groups_total

    first_held, second_held = gather_weights([conv1_weight, conv2_weight])
    first_local = jnp.concatenate(first_held[:2], axis=2)
    first_remote = jnp.concatenate(first_held[2:], axis=2)
    second_local = jnp.concatenate(second_held[:2], axis=2)
    second_remote = jnp.concatenate(second_held[2:], axis=2)
    order = relative_order(channels)

    def expand(values):
        return jnp.repeat(values, per_group, axis=1)[:, None, None, :]

    stacked = jnp.stack([latent_in, cached_mid])
    padded = padded_2(stacked, (("row", 2), ("col", 3)), 1)
    inputs_pad = padded[0].astype(jnp.float32)
    margins_pad = padded[1].astype(jnp.float32)

    row_start = lax.axis_index("row") * rows_dev - 1
    col_start = lax.axis_index("col") * cols_dev - 1
    cell_rows = row_start + jnp.arange(rows_dev + 2, dtype=jnp.int32)
    cell_cols = col_start + jnp.arange(cols_dev + 2, dtype=jnp.int32)
    inside = ((cell_rows >= 0) & (cell_rows < rows_total))[:, None] & (
        (cell_cols >= 0) & (cell_cols < cols_total)
    )[None, :]
    inside = inside.astype(jnp.float32)[None, :, :, None]

    first_act = (
        jax.nn.silu(
            (inputs_pad - expand(norm1_mean)) * expand(norm1_rstd) * norm1_gain + norm1_shift
        )
        * inside
    ).astype(jnp.bfloat16)
    first_moved = to_relative(first_act, order)
    first_split = first_local.shape[2]
    fresh_mid = (
        conv_valid(first_moved[..., :first_split], first_local)
        + conv_valid(first_moved[..., first_split:], first_remote)
        + conv1_bias
        + step_embed[:, None, None, :]
    )

    if tiles_down != 1:
        raise ValueError("tiles_down")
    second_mean = expand(norm2_mean)
    second_rstd = expand(norm2_rstd)

    def second_norm(values):
        return jax.nn.silu((values - second_mean) * second_rstd * norm2_gain + norm2_shift)

    cached_act = to_relative((second_norm(margins_pad) * inside).astype(jnp.bfloat16), order)
    fresh_act = to_relative(second_norm(fresh_mid).astype(jnp.bfloat16), order)
    fresh_pad = jnp.pad(fresh_act, ((0, 0), (1, 1), (1, 1), (0, 0)))
    edge = jnp.arange(TILE + 2, dtype=jnp.int32)
    interior = ((edge >= 1) & (edge <= TILE))[:, None] & ((edge >= 1) & (edge <= TILE))[None, :]
    interior = interior[None, :, :, None]
    windows = []
    for tile_across in range(tiles_across):
        cut = slice(tile_across * TILE, tile_across * TILE + TILE + 2)
        windows.append(jnp.where(interior, fresh_pad[:, :, cut], cached_act[:, :, cut]))
    wide = jnp.concatenate(windows, axis=2)
    split = second_local.shape[2]
    wide_sum = conv_valid(wide[..., :split], second_local) + conv_valid(
        wide[..., split:], second_remote
    )
    stride = TILE + 2
    second_sum = jnp.concatenate(
        [wide_sum[:, :, t * stride : t * stride + TILE] for t in range(tiles_across)], axis=2
    )
    renewed = (
        second_sum + conv2_bias + inputs_pad[:, 1 : 1 + rows_dev, 1 : 1 + cols_dev]
    ).astype(jnp.bfloat16)

    own_rows = lax.axis_index("row") * tiles_down + jnp.arange(tiles_down, dtype=jnp.int32)
    own_cols = lax.axis_index("col") * tiles_across + jnp.arange(tiles_across, dtype=jnp.int32)
    tile_numbers = own_rows[:, None] * tile_cols_total + own_cols[None, :]
    edited = jnp.any(edit_tiles[:, None, None, :] == tile_numbers[None, :, :, None], axis=-1)
    cell_mask = jnp.repeat(jnp.repeat(edited, TILE, axis=1), TILE, axis=2)
    return jnp.where(cell_mask[..., None], renewed, cached_out)


def solution(mesh):
    placed = (
        P("groups", "row", "col", None),
        P("groups", "row", "col", None),
        P("groups", "row", "col", None),
        P("groups", None),
        P("groups", None),
        P("groups", None),
        P(),
        P(),
        P(None, None, "row", None),
        P(),
        P("groups", None),
        P("groups", None),
        P("groups", None),
        P(),
        P(),
        P(None, None, "row", None),
        P(),
    )
    return jax.shard_map(
        body, mesh=mesh, in_specs=placed, out_specs=P("groups", "row", "col", None), check_vma=False
    )
```

```python
import jax
import jax.numpy as jnp
from jax import lax
from jax.sharding import PartitionSpec as P

TILE = 4


def padded_2(block, sides, width):
    for axis, dim in sides:
        count = lax.axis_size(axis)
        forward = [(i, i + 1) for i in range(count - 1)]
        backward = [(target, source) for source, target in forward]
        low = lax.ppermute(
            lax.slice_in_dim(block, block.shape[dim] - width, None, axis=dim), axis, forward
        )
        high = lax.ppermute(lax.slice_in_dim(block, 0, width, axis=dim), axis, backward)
        block = jnp.concatenate([low, block, high], axis=dim)
    return block


def gather_weights(kernels):
    count = lax.axis_size("row")
    chips = count // 2
    y_pairs = [(i, i ^ 1) for i in range(lax.axis_size("groups"))]
    mate_pairs = [(i, i ^ 1) for i in range(count)]
    parity = lax.axis_index("groups") % 2
    wholes = []
    previous = None
    for shard in kernels:
        depth = shard.shape[2]
        halves = shard.reshape(shard.shape[:2] + (2, depth // 2) + shard.shape[3:])
        mine = lax.dynamic_index_in_dim(halves, parity, axis=2, keepdims=False)
        held = [shard, lax.ppermute(shard, "row", mate_pairs)]
        for step in range(1, chips):
            if previous is not None:
                mine, _ = lax.optimization_barrier((mine, previous))
            pairs = [(((i // 2 + step) % chips) * 2 + i % 2, i) for i in range(count)]
            fetched = lax.ppermute(mine, "row", pairs)
            previous = fetched
            other = lax.ppermute(fetched, "groups", y_pairs)
            relayed = lax.ppermute(fetched, "row", mate_pairs)
            other_relayed = lax.ppermute(other, "row", mate_pairs)
            held += [
                jnp.concatenate([fetched, other], axis=2),
                jnp.concatenate([relayed, other_relayed], axis=2),
            ]
        wholes.append(held)
    return wholes


def relative_order(channels):
    count = lax.axis_size("row")
    chips = count // 2
    depth = channels // count
    me = lax.axis_index("row")
    chip = me // 2
    core = me % 2
    position = jnp.arange(channels, dtype=jnp.int32)
    block = position // depth
    within = position % depth
    source = 2 * ((chip + block // 2) % chips) + jnp.where(block % 2 == 0, core, 1 - core)
    half = depth // 2
    parity = lax.axis_index("groups") % 2
    shuffled = (parity ^ (within // half)) * half + within % half
    return source * depth + jnp.where(block >= 2, shuffled, within)


def to_relative(activation, order):
    natural = jnp.arange(activation.shape[-1], dtype=jnp.int32)[:, None]
    chooser = (natural == order[None, :]).astype(activation.dtype)
    moved = jnp.dot(activation, chooser, preferred_element_type=jnp.float32)
    return moved.astype(activation.dtype)


def conv_relative(activation, kernel, order):
    return conv_valid(to_relative(activation, order), kernel)


def conv_parts(activation, kernels):
    total = None
    start = 0
    for kernel in kernels:
        depth = kernel.shape[2]
        part = conv_valid(activation[..., start : start + depth], kernel)
        total = part if total is None else total + part
        start += depth
    return total


def conv_valid(activation, kernel):
    return lax.conv_general_dilated(
        activation,
        kernel,
        window_strides=(1, 1),
        padding="VALID",
        dimension_numbers=("NHWC", "HWIO", "NHWC"),
        preferred_element_type=jnp.float32,
    )


def body(
    latent_in,
    cached_mid,
    cached_out,
    edit_tiles,
    norm1_mean,
    norm1_rstd,
    norm1_gain,
    norm1_shift,
    conv1_weight,
    conv1_bias,
    step_embed,
    norm2_mean,
    norm2_rstd,
    norm2_gain,
    norm2_shift,
    conv2_weight,
    conv2_bias,
):
    requests, rows_dev, cols_dev, channels = latent_in.shape
    tiles_down = rows_dev // TILE
    tiles_across = cols_dev // TILE
    rows_total = rows_dev * lax.axis_size("row")
    cols_total = cols_dev * lax.axis_size("col")
    tile_cols_total = tiles_across * lax.axis_size("col")
    groups_total = norm1_mean.shape[1]
    per_group = channels // groups_total

    first_held, second_held = gather_weights([conv1_weight, conv2_weight])
    first_parts = [jnp.concatenate(first_held[:2], axis=2)] + first_held[2:]
    second_parts = [jnp.concatenate(second_held[:2], axis=2)] + second_held[2:]
    order = relative_order(channels)

    def expand(values):
        return jnp.repeat(values, per_group, axis=1)[:, None, None, :]

    stacked = jnp.stack([latent_in, cached_mid])
    padded = padded_2(stacked, (("row", 2), ("col", 3)), 1)
    inputs_pad = padded[0].astype(jnp.float32)
    margins_pad = padded[1].astype(jnp.float32)

    row_start = lax.axis_index("row") * rows_dev - 1
    col_start = lax.axis_index("col") * cols_dev - 1
    cell_rows = row_start + jnp.arange(rows_dev + 2, dtype=jnp.int32)
    cell_cols = col_start + jnp.arange(cols_dev + 2, dtype=jnp.int32)
    inside = ((cell_rows >= 0) & (cell_rows < rows_total))[:, None] & (
        (cell_cols >= 0) & (cell_cols < cols_total)
    )[None, :]
    inside = inside.astype(jnp.float32)[None, :, :, None]

    first_act = (
        jax.nn.silu(
            (inputs_pad - expand(norm1_mean)) * expand(norm1_rstd) * norm1_gain + norm1_shift
        )
        * inside
    ).astype(jnp.bfloat16)
    first_moved = to_relative(first_act, order)
    fresh_mid = (
        conv_parts(first_moved, first_parts)
        + conv1_bias
        + step_embed[:, None, None, :]
    )

    if tiles_down != 1:
        raise ValueError("tiles_down")
    second_mean = expand(norm2_mean)
    second_rstd = expand(norm2_rstd)

    def second_norm(values):
        return jax.nn.silu((values - second_mean) * second_rstd * norm2_gain + norm2_shift)

    cached_act = to_relative((second_norm(margins_pad) * inside).astype(jnp.bfloat16), order)
    fresh_act = to_relative(second_norm(fresh_mid).astype(jnp.bfloat16), order)
    fresh_pad = jnp.pad(fresh_act, ((0, 0), (1, 1), (1, 1), (0, 0)))
    edge = jnp.arange(TILE + 2, dtype=jnp.int32)
    interior = ((edge >= 1) & (edge <= TILE))[:, None] & ((edge >= 1) & (edge <= TILE))[None, :]
    interior = interior[None, :, :, None]
    windows = []
    for tile_across in range(tiles_across):
        cut = slice(tile_across * TILE, tile_across * TILE + TILE + 2)
        windows.append(jnp.where(interior, fresh_pad[:, :, cut], cached_act[:, :, cut]))
    wide = jnp.concatenate(windows, axis=2)
    wide_sum = conv_parts(wide, second_parts)
    stride = TILE + 2
    second_sum = jnp.concatenate(
        [wide_sum[:, :, t * stride : t * stride + TILE] for t in range(tiles_across)], axis=2
    )
    renewed = (
        second_sum + conv2_bias + inputs_pad[:, 1 : 1 + rows_dev, 1 : 1 + cols_dev]
    ).astype(jnp.bfloat16)

    own_rows = lax.axis_index("row") * tiles_down + jnp.arange(tiles_down, dtype=jnp.int32)
    own_cols = lax.axis_index("col") * tiles_across + jnp.arange(tiles_across, dtype=jnp.int32)
    tile_numbers = own_rows[:, None] * tile_cols_total + own_cols[None, :]
    edited = jnp.any(edit_tiles[:, None, None, :] == tile_numbers[None, :, :, None], axis=-1)
    cell_mask = jnp.repeat(jnp.repeat(edited, TILE, axis=1), TILE, axis=2)
    return jnp.where(cell_mask[..., None], renewed, cached_out)


def solution(mesh):
    placed = (
        P("groups", "row", "col", None),
        P("groups", "row", "col", None),
        P("groups", "row", "col", None),
        P("groups", None),
        P("groups", None),
        P("groups", None),
        P(),
        P(),
        P(None, None, "row", None),
        P(),
        P("groups", None),
        P("groups", None),
        P("groups", None),
        P(),
        P(),
        P(None, None, "row", None),
        P(),
    )
    return jax.shard_map(
        body, mesh=mesh, in_specs=placed, out_specs=P("groups", "row", "col", None), check_vma=False
    )
```

```python
import jax
import jax.numpy as jnp
from jax import lax
from jax.sharding import PartitionSpec as P

TILE = 4


def padded_2(block, sides, width):
    for axis, dim in sides:
        count = lax.axis_size(axis)
        forward = [(i, i + 1) for i in range(count - 1)]
        backward = [(target, source) for source, target in forward]
        low = lax.ppermute(
            lax.slice_in_dim(block, block.shape[dim] - width, None, axis=dim), axis, forward
        )
        high = lax.ppermute(lax.slice_in_dim(block, 0, width, axis=dim), axis, backward)
        block = jnp.concatenate([low, block, high], axis=dim)
    return block


def gather_weights(kernels):
    count = lax.axis_size("row")
    chips = count // 2
    y_pairs = [(i, i ^ 1) for i in range(lax.axis_size("groups"))]
    mate_pairs = [(i, i ^ 1) for i in range(count)]
    parity = lax.axis_index("groups") % 2
    wholes = []
    previous = None
    for shard in kernels:
        depth = shard.shape[2]
        halves = shard.reshape(shard.shape[:2] + (2, depth // 2) + shard.shape[3:])
        mine = lax.dynamic_index_in_dim(halves, parity, axis=2, keepdims=False)
        held = [shard, lax.ppermute(shard, "row", mate_pairs)]
        for step in range(1, chips):
            if previous is not None:
                mine, _ = lax.optimization_barrier((mine, previous))
            pairs = [(((i // 2 + step) % chips) * 2 + i % 2, i) for i in range(count)]
            fetched = lax.ppermute(mine, "row", pairs)
            previous = fetched
            other = lax.ppermute(fetched, "groups", y_pairs)
            relayed = lax.ppermute(fetched, "row", mate_pairs)
            other_relayed = lax.ppermute(other, "row", mate_pairs)
            held += [
                jnp.concatenate([fetched, other], axis=2),
                jnp.concatenate([relayed, other_relayed], axis=2),
            ]
        wholes.append(held)
    return wholes


def relative_order(channels):
    count = lax.axis_size("row")
    chips = count // 2
    depth = channels // count
    me = lax.axis_index("row")
    chip = me // 2
    core = me % 2
    position = jnp.arange(channels, dtype=jnp.int32)
    block = position // depth
    within = position % depth
    source = 2 * ((chip + block // 2) % chips) + jnp.where(block % 2 == 0, core, 1 - core)
    half = depth // 2
    parity = lax.axis_index("groups") % 2
    shuffled = (parity ^ (within // half)) * half + within % half
    return source * depth + jnp.where(block >= 2, shuffled, within)


def to_relative(activation, order):
    natural = jnp.arange(activation.shape[-1], dtype=jnp.int32)[:, None]
    chooser = (natural == order[None, :]).astype(activation.dtype)
    return jnp.dot(activation, chooser, preferred_element_type=activation.dtype)


def conv_relative(activation, kernel, order):
    return conv_valid(to_relative(activation, order), kernel)


def conv_valid(activation, kernel):
    return lax.conv_general_dilated(
        activation,
        kernel,
        window_strides=(1, 1),
        padding="VALID",
        dimension_numbers=("NHWC", "HWIO", "NHWC"),
        preferred_element_type=jnp.float32,
    )


def body(
    latent_in,
    cached_mid,
    cached_out,
    edit_tiles,
    norm1_mean,
    norm1_rstd,
    norm1_gain,
    norm1_shift,
    conv1_weight,
    conv1_bias,
    step_embed,
    norm2_mean,
    norm2_rstd,
    norm2_gain,
    norm2_shift,
    conv2_weight,
    conv2_bias,
):
    requests, rows_dev, cols_dev, channels = latent_in.shape
    tiles_down = rows_dev // TILE
    tiles_across = cols_dev // TILE
    rows_total = rows_dev * lax.axis_size("row")
    cols_total = cols_dev * lax.axis_size("col")
    tile_cols_total = tiles_across * lax.axis_size("col")
    groups_total = norm1_mean.shape[1]
    per_group = channels // groups_total

    first_held, second_held = gather_weights([conv1_weight, conv2_weight])
    first_local = jnp.concatenate(first_held[:2], axis=2)
    first_remote = jnp.concatenate(first_held[2:], axis=2)
    second_local = jnp.concatenate(second_held[:2], axis=2)
    second_remote = jnp.concatenate(second_held[2:], axis=2)
    order = relative_order(channels)

    def expand(values):
        return jnp.repeat(values, per_group, axis=1)[:, None, None, :]

    stacked = jnp.stack([latent_in, cached_mid])
    padded = padded_2(stacked, (("row", 2), ("col", 3)), 1)
    inputs_pad = padded[0].astype(jnp.float32)
    margins_pad = padded[1].astype(jnp.float32)

    row_start = lax.axis_index("row") * rows_dev - 1
    col_start = lax.axis_index("col") * cols_dev - 1
    cell_rows = row_start + jnp.arange(rows_dev + 2, dtype=jnp.int32)
    cell_cols = col_start + jnp.arange(cols_dev + 2, dtype=jnp.int32)
    inside = ((cell_rows >= 0) & (cell_rows < rows_total))[:, None] & (
        (cell_cols >= 0) & (cell_cols < cols_total)
    )[None, :]
    inside = inside.astype(jnp.float32)[None, :, :, None]

    first_act = (
        jax.nn.silu(
            (inputs_pad - expand(norm1_mean)) * expand(norm1_rstd) * norm1_gain + norm1_shift
        )
        * inside
    ).astype(jnp.bfloat16)
    first_moved = to_relative(first_act, order)
    first_split = first_local.shape[2]
    fresh_mid = (
        conv_valid(first_moved[..., :first_split], first_local)
        + conv_valid(first_moved[..., first_split:], first_remote)
        + conv1_bias
        + step_embed[:, None, None, :]
    )

    if tiles_down != 1:
        raise ValueError("tiles_down")
    second_mean = expand(norm2_mean)
    second_rstd = expand(norm2_rstd)

    def second_norm(values):
        return jax.nn.silu((values - second_mean) * second_rstd * norm2_gain + norm2_shift)

    cached_act = to_relative((second_norm(margins_pad) * inside).astype(jnp.bfloat16), order)
    fresh_act = to_relative(second_norm(fresh_mid).astype(jnp.bfloat16), order)
    fresh_pad = jnp.pad(fresh_act, ((0, 0), (1, 1), (1, 1), (0, 0)))
    edge = jnp.arange(TILE + 2, dtype=jnp.int32)
    interior = ((edge >= 1) & (edge <= TILE))[:, None] & ((edge >= 1) & (edge <= TILE))[None, :]
    interior = interior[None, :, :, None]
    windows = []
    for tile_across in range(tiles_across):
        cut = slice(tile_across * TILE, tile_across * TILE + TILE + 2)
        windows.append(jnp.where(interior, fresh_pad[:, :, cut], cached_act[:, :, cut]))
    wide = jnp.concatenate(windows, axis=2)
    split = second_local.shape[2]
    wide_sum = conv_valid(wide[..., :split], second_local) + conv_valid(
        wide[..., split:], second_remote
    )
    stride = TILE + 2
    second_sum = jnp.concatenate(
        [wide_sum[:, :, t * stride : t * stride + TILE] for t in range(tiles_across)], axis=2
    )
    renewed = (
        second_sum + conv2_bias + inputs_pad[:, 1 : 1 + rows_dev, 1 : 1 + cols_dev]
    ).astype(jnp.bfloat16)

    own_rows = lax.axis_index("row") * tiles_down + jnp.arange(tiles_down, dtype=jnp.int32)
    own_cols = lax.axis_index("col") * tiles_across + jnp.arange(tiles_across, dtype=jnp.int32)
    tile_numbers = own_rows[:, None] * tile_cols_total + own_cols[None, :]
    edited = jnp.any(edit_tiles[:, None, None, :] == tile_numbers[None, :, :, None], axis=-1)
    cell_mask = jnp.repeat(jnp.repeat(edited, TILE, axis=1), TILE, axis=2)
    return jnp.where(cell_mask[..., None], renewed, cached_out)


def solution(mesh):
    placed = (
        P("groups", "row", "col", None),
        P("groups", "row", "col", None),
        P("groups", "row", "col", None),
        P("groups", None),
        P("groups", None),
        P("groups", None),
        P(),
        P(),
        P(None, None, "row", None),
        P(),
        P("groups", None),
        P("groups", None),
        P("groups", None),
        P(),
        P(),
        P(None, None, "row", None),
        P(),
    )
    return jax.shard_map(
        body, mesh=mesh, in_specs=placed, out_specs=P("groups", "row", "col", None), check_vma=False
    )
```

```python
import jax
import jax.numpy as jnp
from jax import lax
from jax.sharding import PartitionSpec as P

TILE = 4


def padded_2(block, sides, width):
    for axis, dim in sides:
        count = lax.axis_size(axis)
        forward = [(i, i + 1) for i in range(count - 1)]
        backward = [(target, source) for source, target in forward]
        low = lax.ppermute(
            lax.slice_in_dim(block, block.shape[dim] - width, None, axis=dim), axis, forward
        )
        high = lax.ppermute(lax.slice_in_dim(block, 0, width, axis=dim), axis, backward)
        block = jnp.concatenate([low, block, high], axis=dim)
    return block


def gather_weights(kernels):
    count = lax.axis_size("row")
    chips = count // 2
    y_pairs = [(i, i ^ 1) for i in range(lax.axis_size("groups"))]
    mate_pairs = [(i, i ^ 1) for i in range(count)]
    parity = lax.axis_index("groups") % 2
    wholes = []
    previous = None
    for shard in kernels:
        depth = shard.shape[2]
        halves = shard.reshape(shard.shape[:2] + (2, depth // 2) + shard.shape[3:])
        mine = lax.dynamic_index_in_dim(halves, parity, axis=2, keepdims=False)
        held = [shard, lax.ppermute(shard, "row", mate_pairs)]
        for step in range(1, chips):
            if previous is not None:
                mine, _ = lax.optimization_barrier((mine, previous))
            pairs = [(((i // 2 + step) % chips) * 2 + i % 2, i) for i in range(count)]
            fetched = lax.ppermute(mine, "row", pairs)
            previous = fetched
            other = lax.ppermute(fetched, "groups", y_pairs)
            relayed = lax.ppermute(fetched, "row", mate_pairs)
            other_relayed = lax.ppermute(other, "row", mate_pairs)
            held += [
                jnp.concatenate([fetched, other], axis=2),
                jnp.concatenate([relayed, other_relayed], axis=2),
            ]
        wholes.append(held)
    return wholes


def relative_order(channels):
    count = lax.axis_size("row")
    chips = count // 2
    depth = channels // count
    me = lax.axis_index("row")
    chip = me // 2
    core = me % 2
    position = jnp.arange(channels, dtype=jnp.int32)
    block = position // depth
    within = position % depth
    source = 2 * ((chip + block // 2) % chips) + jnp.where(block % 2 == 0, core, 1 - core)
    half = depth // 2
    parity = lax.axis_index("groups") % 2
    shuffled = (parity ^ (within // half)) * half + within % half
    return source * depth + jnp.where(block >= 2, shuffled, within)


def to_relative(activation, order):
    natural = jnp.arange(activation.shape[-1], dtype=jnp.int32)[:, None]
    chooser = (natural == order[None, :]).astype(activation.dtype)
    moved = jnp.dot(activation, chooser, preferred_element_type=jnp.float32)
    return moved.astype(activation.dtype)


def conv_relative(activation, kernel, order):
    return conv_valid(to_relative(activation, order), kernel)


def conv_valid(activation, kernel):
    return lax.conv_general_dilated(
        activation,
        kernel,
        window_strides=(1, 1),
        padding="VALID",
        dimension_numbers=("NHWC", "HWIO", "NHWC"),
        preferred_element_type=jnp.float32,
    )


def body(
    latent_in,
    cached_mid,
    cached_out,
    edit_tiles,
    norm1_mean,
    norm1_rstd,
    norm1_gain,
    norm1_shift,
    conv1_weight,
    conv1_bias,
    step_embed,
    norm2_mean,
    norm2_rstd,
    norm2_gain,
    norm2_shift,
    conv2_weight,
    conv2_bias,
):
    requests, rows_dev, cols_dev, channels = latent_in.shape
    tiles_down = rows_dev // TILE
    tiles_across = cols_dev // TILE
    rows_total = rows_dev * lax.axis_size("row")
    cols_total = cols_dev * lax.axis_size("col")
    tile_cols_total = tiles_across * lax.axis_size("col")
    groups_total = norm1_mean.shape[1]
    per_group = channels // groups_total

    first_held, second_held = gather_weights([conv1_weight, conv2_weight])
    first_local = jnp.concatenate(first_held[:2], axis=2)
    first_remote = jnp.concatenate(first_held[2:], axis=2)
    second_local = jnp.concatenate(second_held[:2], axis=2)
    second_remote = jnp.concatenate(second_held[2:], axis=2)
    order = relative_order(channels)

    def expand(values):
        return jnp.repeat(values, per_group, axis=1)[:, None, None, :]

    stacked = jnp.stack([latent_in, cached_mid])
    padded = padded_2(stacked, (("row", 2), ("col", 3)), 1)
    inputs_pad = padded[0].astype(jnp.float32)
    margins_pad = padded[1].astype(jnp.float32)

    row_start = lax.axis_index("row") * rows_dev - 1
    col_start = lax.axis_index("col") * cols_dev - 1
    cell_rows = row_start + jnp.arange(rows_dev + 2, dtype=jnp.int32)
    cell_cols = col_start + jnp.arange(cols_dev + 2, dtype=jnp.int32)
    inside = ((cell_rows >= 0) & (cell_rows < rows_total))[:, None] & (
        (cell_cols >= 0) & (cell_cols < cols_total)
    )[None, :]
    inside = inside.astype(jnp.float32)[None, :, :, None]

    first_act = (
        jax.nn.silu(
            (inputs_pad - expand(norm1_mean)) * expand(norm1_rstd) * norm1_gain + norm1_shift
        )
        * inside
    ).astype(jnp.bfloat16)
    first_moved = to_relative(first_act, order)
    first_split = first_local.shape[2]
    fresh_mid = (
        conv_valid(first_moved[..., :first_split], first_local)
        + conv_valid(first_moved[..., first_split:], first_remote)
        + conv1_bias
        + step_embed[:, None, None, :]
    )

    if tiles_down != 1:
        raise ValueError("tiles_down")
    second_mean = expand(norm2_mean)
    second_rstd = expand(norm2_rstd)

    def second_norm(values):
        return jax.nn.silu((values - second_mean) * second_rstd * norm2_gain + norm2_shift)

    cached_norm = (second_norm(margins_pad) * inside).astype(jnp.bfloat16)
    fresh_norm = second_norm(fresh_mid).astype(jnp.bfloat16)
    edge = jnp.arange(TILE + 2, dtype=jnp.int32)
    interior = ((edge >= 1) & (edge <= TILE))[:, None] & ((edge >= 1) & (edge <= TILE))[None, :]
    interior = interior[None, :, :, None]
    split = second_local.shape[2]
    wide_sum = None
    for kernel, picks in ((second_local, order[:split]), (second_remote, order[split:])):
        cached_act = to_relative(cached_norm, picks)
        fresh_pad = jnp.pad(to_relative(fresh_norm, picks), ((0, 0), (1, 1), (1, 1), (0, 0)))
        windows = []
        for tile_across in range(tiles_across):
            cut = slice(tile_across * TILE, tile_across * TILE + TILE + 2)
            windows.append(jnp.where(interior, fresh_pad[:, :, cut], cached_act[:, :, cut]))
        part = conv_valid(jnp.concatenate(windows, axis=2), kernel)
        wide_sum = part if wide_sum is None else wide_sum + part
    stride = TILE + 2
    second_sum = jnp.concatenate(
        [wide_sum[:, :, t * stride : t * stride + TILE] for t in range(tiles_across)], axis=2
    )
    renewed = (
        second_sum + conv2_bias + inputs_pad[:, 1 : 1 + rows_dev, 1 : 1 + cols_dev]
    ).astype(jnp.bfloat16)

    own_rows = lax.axis_index("row") * tiles_down + jnp.arange(tiles_down, dtype=jnp.int32)
    own_cols = lax.axis_index("col") * tiles_across + jnp.arange(tiles_across, dtype=jnp.int32)
    tile_numbers = own_rows[:, None] * tile_cols_total + own_cols[None, :]
    edited = jnp.any(edit_tiles[:, None, None, :] == tile_numbers[None, :, :, None], axis=-1)
    cell_mask = jnp.repeat(jnp.repeat(edited, TILE, axis=1), TILE, axis=2)
    return jnp.where(cell_mask[..., None], renewed, cached_out)


def solution(mesh):
    placed = (
        P("groups", "row", "col", None),
        P("groups", "row", "col", None),
        P("groups", "row", "col", None),
        P("groups", None),
        P("groups", None),
        P("groups", None),
        P(),
        P(),
        P(None, None, "row", None),
        P(),
        P("groups", None),
        P("groups", None),
        P("groups", None),
        P(),
        P(),
        P(None, None, "row", None),
        P(),
    )
    return jax.shard_map(
        body, mesh=mesh, in_specs=placed, out_specs=P("groups", "row", "col", None), check_vma=False
    )
```

```python
import jax
import jax.numpy as jnp
from jax import lax
from jax.sharding import PartitionSpec as P

TILE = 4


def padded_2(block, sides, width):
    for axis, dim in sides:
        count = lax.axis_size(axis)
        forward = [(i, i + 1) for i in range(count - 1)]
        backward = [(target, source) for source, target in forward]
        low = lax.ppermute(
            lax.slice_in_dim(block, block.shape[dim] - width, None, axis=dim), axis, forward
        )
        high = lax.ppermute(lax.slice_in_dim(block, 0, width, axis=dim), axis, backward)
        block = jnp.concatenate([low, block, high], axis=dim)
    return block


def gather_weights(kernels):
    count = lax.axis_size("row")
    chips = count // 2
    y_pairs = [(i, i ^ 1) for i in range(lax.axis_size("groups"))]
    mate_pairs = [(i, i ^ 1) for i in range(count)]
    parity = lax.axis_index("groups") % 2
    wholes = []
    for shard in kernels:
        depth = shard.shape[2]
        halves = shard.reshape(shard.shape[:2] + (2, depth // 2) + shard.shape[3:])
        mine = lax.dynamic_index_in_dim(halves, parity, axis=2, keepdims=False)
        held = [shard, lax.ppermute(shard, "row", mate_pairs)]
        for step in range(1, chips):
            pairs = [(((i // 2 + step) % chips) * 2 + i % 2, i) for i in range(count)]
            fetched = lax.ppermute(mine, "row", pairs)
            other = lax.ppermute(fetched, "groups", y_pairs)
            relayed = lax.ppermute(fetched, "row", mate_pairs)
            other_relayed = lax.ppermute(other, "row", mate_pairs)
            held += [
                jnp.concatenate([fetched, other], axis=2),
                jnp.concatenate([relayed, other_relayed], axis=2),
            ]
        wholes.append(held)
    return wholes


def relative_order(channels):
    count = lax.axis_size("row")
    chips = count // 2
    depth = channels // count
    me = lax.axis_index("row")
    chip = me // 2
    core = me % 2
    position = jnp.arange(channels, dtype=jnp.int32)
    block = position // depth
    within = position % depth
    source = 2 * ((chip + block // 2) % chips) + jnp.where(block % 2 == 0, core, 1 - core)
    half = depth // 2
    parity = lax.axis_index("groups") % 2
    shuffled = (parity ^ (within // half)) * half + within % half
    return source * depth + jnp.where(block >= 2, shuffled, within)


def to_relative(activation, order):
    natural = jnp.arange(activation.shape[-1], dtype=jnp.int32)[:, None]
    chooser = (natural == order[None, :]).astype(activation.dtype)
    moved = jnp.dot(activation, chooser, preferred_element_type=jnp.float32)
    return moved.astype(activation.dtype)


def conv_relative(activation, kernel, order):
    return conv_valid(to_relative(activation, order), kernel)


def conv_valid(activation, kernel):
    return lax.conv_general_dilated(
        activation,
        kernel,
        window_strides=(1, 1),
        padding="VALID",
        dimension_numbers=("NHWC", "HWIO", "NHWC"),
        preferred_element_type=jnp.float32,
    )


def body(
    latent_in,
    cached_mid,
    cached_out,
    edit_tiles,
    norm1_mean,
    norm1_rstd,
    norm1_gain,
    norm1_shift,
    conv1_weight,
    conv1_bias,
    step_embed,
    norm2_mean,
    norm2_rstd,
    norm2_gain,
    norm2_shift,
    conv2_weight,
    conv2_bias,
):
    requests, rows_dev, cols_dev, channels = latent_in.shape
    tiles_down = rows_dev // TILE
    tiles_across = cols_dev // TILE
    rows_total = rows_dev * lax.axis_size("row")
    cols_total = cols_dev * lax.axis_size("col")
    tile_cols_total = tiles_across * lax.axis_size("col")
    groups_total = norm1_mean.shape[1]
    per_group = channels // groups_total

    first_held, second_held = gather_weights([conv1_weight, conv2_weight])
    first_local = jnp.concatenate(first_held[:2], axis=2)
    first_remote = jnp.concatenate(first_held[2:], axis=2)
    second_local = jnp.concatenate(second_held[:2], axis=2)
    second_remote = jnp.concatenate(second_held[2:], axis=2)
    order = relative_order(channels)

    def expand(values):
        return jnp.repeat(values, per_group, axis=1)[:, None, None, :]

    stacked = jnp.stack([latent_in, cached_mid])
    padded = padded_2(stacked, (("row", 2), ("col", 3)), 1)
    inputs_pad = padded[0].astype(jnp.float32)
    margins_pad = padded[1].astype(jnp.float32)

    row_start = lax.axis_index("row") * rows_dev - 1
    col_start = lax.axis_index("col") * cols_dev - 1
    cell_rows = row_start + jnp.arange(rows_dev + 2, dtype=jnp.int32)
    cell_cols = col_start + jnp.arange(cols_dev + 2, dtype=jnp.int32)
    inside = ((cell_rows >= 0) & (cell_rows < rows_total))[:, None] & (
        (cell_cols >= 0) & (cell_cols < cols_total)
    )[None, :]
    inside = inside.astype(jnp.float32)[None, :, :, None]

    first_act = (
        jax.nn.silu(
            (inputs_pad - expand(norm1_mean)) * expand(norm1_rstd) * norm1_gain + norm1_shift
        )
        * inside
    ).astype(jnp.bfloat16)
    first_moved = to_relative(first_act, order)
    first_split = first_local.shape[2]
    fresh_mid = (
        conv_valid(first_moved[..., :first_split], first_local)
        + conv_valid(first_moved[..., first_split:], first_remote)
        + conv1_bias
        + step_embed[:, None, None, :]
    )

    if tiles_down != 1:
        raise ValueError("tiles_down")
    second_mean = expand(norm2_mean)
    second_rstd = expand(norm2_rstd)

    def second_norm(values):
        return jax.nn.silu((values - second_mean) * second_rstd * norm2_gain + norm2_shift)

    cached_act = to_relative((second_norm(margins_pad) * inside).astype(jnp.bfloat16), order)
    fresh_act = to_relative(second_norm(fresh_mid).astype(jnp.bfloat16), order)
    fresh_pad = jnp.pad(fresh_act, ((0, 0), (1, 1), (1, 1), (0, 0)))
    edge = jnp.arange(TILE + 2, dtype=jnp.int32)
    interior = ((edge >= 1) & (edge <= TILE))[:, None] & ((edge >= 1) & (edge <= TILE))[None, :]
    interior = interior[None, :, :, None]
    windows = []
    for tile_across in range(tiles_across):
        cut = slice(tile_across * TILE, tile_across * TILE + TILE + 2)
        windows.append(jnp.where(interior, fresh_pad[:, :, cut], cached_act[:, :, cut]))
    wide = jnp.concatenate(windows, axis=2)
    split = second_local.shape[2]
    wide_sum = conv_valid(wide[..., :split], second_local) + conv_valid(
        wide[..., split:], second_remote
    )
    stride = TILE + 2
    second_sum = jnp.concatenate(
        [wide_sum[:, :, t * stride : t * stride + TILE] for t in range(tiles_across)], axis=2
    )
    renewed = (
        second_sum + conv2_bias + inputs_pad[:, 1 : 1 + rows_dev, 1 : 1 + cols_dev]
    ).astype(jnp.bfloat16)

    own_rows = lax.axis_index("row") * tiles_down + jnp.arange(tiles_down, dtype=jnp.int32)
    own_cols = lax.axis_index("col") * tiles_across + jnp.arange(tiles_across, dtype=jnp.int32)
    tile_numbers = own_rows[:, None] * tile_cols_total + own_cols[None, :]
    edited = jnp.any(edit_tiles[:, None, None, :] == tile_numbers[None, :, :, None], axis=-1)
    cell_mask = jnp.repeat(jnp.repeat(edited, TILE, axis=1), TILE, axis=2)
    return jnp.where(cell_mask[..., None], renewed, cached_out)


def solution(mesh):
    placed = (
        P("groups", "row", "col", None),
        P("groups", "row", "col", None),
        P("groups", "row", "col", None),
        P("groups", None),
        P("groups", None),
        P("groups", None),
        P(),
        P(),
        P(None, None, "row", None),
        P(),
        P("groups", None),
        P("groups", None),
        P("groups", None),
        P(),
        P(),
        P(None, None, "row", None),
        P(),
    )
    return jax.shard_map(
        body, mesh=mesh, in_specs=placed, out_specs=P("groups", "row", "col", None), check_vma=False
    )
```
